32 devices in a mesh: ctx: 8 (over y, x, core), head: 4 (over z).
Axes of the slice: x: 2, y: 2, z: 4, core: 2. Of those that a mesh axis runs over, the one named last changes fastest.
Arguments:
- queries: bfloat16 [4096, 4096], P(('ctx', 'head')), may hold values from -42 to 42
- keys: bfloat16 [4096, 1024], P(('ctx', 'head')), may hold values from -4 to 4
- values: bfloat16 [4096, 1024], P(('ctx', 'head')), may hold values from -6 to 6
- out_grad: bfloat16 [4096, 4096], P(('ctx', 'head')), may hold values from -6 to 6
- beacon_pos: int32 [8, 64], P('ctx'), may hold values from 0 to 511, as said below
Outputs:
- attended: bfloat16 [4096, 4096], P(('ctx', 'head'))
- query_grad: bfloat16 [4096, 4096], P(('ctx', 'head'))
- key_grad: bfloat16 [4096, 1024], P(('ctx', 'head'))
- value_grad: bfloat16 [4096, 1024], P(('ctx', 'head'))
The draws below stay inside these ranges and needn't reach their ends.
Inputs may be any that keep to these rules, and one draw needn't show every extreme that they name: `beacon_pos`: row c holds 64 distinct positions in increasing order, the first equal to 0 and the last equal to 511.
All inputs are finite; a program needn't handle non-finite values.
Results may differ from the reference program's by a relative error of at most 0.029.
Values may be sent and summed in bfloat16 or wider, within the bound.
No kernel may reach another device: no remote copies, remote signals or barrier semaphores. Data moves between devices by JAX's collectives and lax.ppermute only.
A program may use at most 128 MiB of HBM per device.

```python
import jax
import jax.numpy as jnp
from jax import lax

HEADS = 32
KV_HEADS = 8
HD = 128
WIN = 512
BEACONS = 64
SHARDS = 8
TOKENS = 4096


def draw_pair(key):
    base = jax.random.fold_in(key, 11)
    key_first, key_second = jax.random.split(base)
    key_vals = jnp.clip(jax.random.normal(key_first, (TOKENS, KV_HEADS * HD), jnp.float32), -4.0, 4.0)
    query_vals = jnp.clip(jax.random.normal(key_second, (TOKENS, HEADS * HD), jnp.float32), -4.0, 4.0)
    return (query_vals, key_vals)


def draw_queries(key, part):
    return draw_pair(key)[0].astype(jnp.bfloat16)


def draw_keys(key, part):
    return draw_pair(key)[1].astype(jnp.bfloat16)


def draw_beacon_pos(key, part):
    row_keys = jax.random.split(jax.random.fold_in(key, 3), SHARDS)

    def one_row(row_key):
        picks = (jax.random.permutation(row_key, WIN - 2)[:BEACONS - 2] + 1).astype(jnp.int32)
        return jnp.concatenate([jnp.zeros((1,), jnp.int32), jnp.sort(picks), jnp.full((1,), WIN - 1, jnp.int32)])
    return jax.vmap(one_row)(row_keys)


def level_of(rng, shape, cuts, low, high):
    level = 1.0
    for axis_at, blocks in cuts:
        draws = jax.random.uniform(jax.random.fold_in(jax.random.fold_in(rng, 6), axis_at), (blocks,), jnp.float32, low / len(cuts), high / len(cuts))
        level = level * jnp.repeat(jnp.exp(draws), shape[axis_at] // blocks).reshape((-1,) + (1,) * (len(shape) - 1 - axis_at))
    return level


def scatter_about(key, extent, deviation, reach, cuts=(), held_as=jnp.bfloat16):
    entries = deviation * jax.random.normal(key, extent, jnp.float32)
    if cuts:
        entries = entries * level_of(key, extent, cuts, -0.22, 0.18)
    return jnp.clip(entries, -reach, reach).astype(held_as)


def setup_inputs(seed: int = 0) -> dict:
    key_list = jax.random.split(jax.random.key(seed), 6)
    return {
        "queries": draw_queries(jax.random.fold_in(key_list[5], 71), 0),
        "keys": draw_keys(jax.random.fold_in(key_list[5], 71), 0),
        "values": scatter_about(key_list[2], (TOKENS, KV_HEADS * HD), 1.0, 6.0, ((0, 32),)),
        "out_grad": scatter_about(key_list[3], (TOKENS, HEADS * HD), 1.0, 6.0, ((0, 32),)),
        "beacon_pos": draw_beacon_pos(jax.random.fold_in(key_list[5], 71), 0),
    }


NEG_FILL = -1e30


def attend(query_group, grad_group, keys_all, values_all, visible):
    scaling = HD ** -0.5
    scores = jnp.einsum("gwd,kd->gwk", query_group.astype(jnp.float32), keys_all.astype(jnp.float32)) * scaling
    scores = jnp.where(visible[None], scores, NEG_FILL)
    row_max = jnp.max(scores, axis=-1, keepdims=True)
    weights = jnp.exp(scores - row_max)
    probabilities = weights / jnp.sum(weights, axis=-1, keepdims=True)
    reduced_probability = probabilities.astype(jnp.bfloat16)
    attended = jnp.einsum("gwk,kd->gwd", reduced_probability.astype(jnp.float32), values_all.astype(jnp.float32)).astype(jnp.bfloat16)
    row_dot = jnp.sum(grad_group.astype(jnp.float32) * attended.astype(jnp.float32), axis=-1, keepdims=True)
    dprob = jnp.einsum("gwd,kd->gwk", grad_group.astype(jnp.float32), values_all.astype(jnp.float32))
    score_gradient = (probabilities * (dprob - row_dot)).astype(jnp.bfloat16)
    query_grad = (jnp.einsum("gwk,kd->gwd", score_gradient.astype(jnp.float32), keys_all.astype(jnp.float32)) * scaling).astype(jnp.bfloat16)
    key_grad = jnp.einsum("gwk,gwd->kd", score_gradient.astype(jnp.float32), query_group.astype(jnp.float32)) * scaling
    value_grad = jnp.einsum("gwk,gwd->kd", reduced_probability.astype(jnp.float32), grad_group.astype(jnp.float32))
    return attended, query_grad, key_grad, value_grad


def reference(queries, keys, values, out_grad, beacon_pos):
    group_size = HEADS // KV_HEADS
    beacon_total = SHARDS * BEACONS
    query_split = queries.reshape(SHARDS, WIN, KV_HEADS, group_size, HD)
    grad_split = out_grad.reshape(SHARDS, WIN, KV_HEADS, group_size, HD)
    key_split = keys.reshape(SHARDS, WIN, KV_HEADS, HD)
    value_split = values.reshape(SHARDS, WIN, KV_HEADS, HD)
    beacon_index = (jnp.arange(SHARDS, dtype=jnp.int32)[:, None] * WIN + beacon_pos.astype(jnp.int32)).reshape(-1)
    beacon_keys = keys[beacon_index].reshape(beacon_total, KV_HEADS, HD).transpose(1, 0, 2)
    beacon_values = values[beacon_index].reshape(beacon_total, KV_HEADS, HD).transpose(1, 0, 2)
    owners = jnp.arange(beacon_total, dtype=jnp.int32) // BEACONS
    causal = jnp.arange(WIN)[:, None] >= jnp.arange(WIN)[None, :]

    def per_shard(carried, shard_id):
        sum_keys, sum_values = carried
        visible = jnp.concatenate([causal, jnp.broadcast_to((owners < shard_id)[None, :], (WIN, beacon_total))], axis=1)
        query_group = query_split[shard_id].transpose(1, 2, 0, 3)
        grad_group = grad_split[shard_id].transpose(1, 2, 0, 3)
        local_keys = key_split[shard_id].transpose(1, 0, 2)
        local_values = value_split[shard_id].transpose(1, 0, 2)

        def per_group(inputs):
            q_part, g_part, k_part, v_part, kb_part, vb_part = inputs
            return attend(q_part, g_part, jnp.concatenate([k_part, kb_part], axis=0), jnp.concatenate([v_part, vb_part], axis=0), visible)

        attended, query_grad, key_grad, value_grad = lax.map(per_group, (query_group, grad_group, local_keys, local_values, beacon_keys, beacon_values))
        sum_keys = sum_keys + key_grad[:, WIN:]
        sum_values = sum_values + value_grad[:, WIN:]
        own_keys = lax.dynamic_slice_in_dim(sum_keys, shard_id * BEACONS, BEACONS, 1)
        own_values = lax.dynamic_slice_in_dim(sum_values, shard_id * BEACONS, BEACONS, 1)
        positions = beacon_pos[shard_id].astype(jnp.int32)
        local_key_grad = key_grad[:, :WIN].at[:, positions].add(own_keys)
        local_value_grad = value_grad[:, :WIN].at[:, positions].add(own_values)
        return (sum_keys, sum_values), (attended, query_grad, local_key_grad.astype(jnp.bfloat16), local_value_grad.astype(jnp.bfloat16))

    initial = (jnp.zeros((KV_HEADS, beacon_total, HD), jnp.float32), jnp.zeros((KV_HEADS, beacon_total, HD), jnp.float32))
    finished, stacked = lax.scan(per_shard, initial, jnp.arange(SHARDS, dtype=jnp.int32), reverse=True)
    attended, query_grad, key_grad, value_grad = stacked
    attended = attended.transpose(0, 3, 1, 2, 4).reshape(TOKENS, HEADS * HD)
    query_grad = query_grad.transpose(0, 3, 1, 2, 4).reshape(TOKENS, HEADS * HD)
    key_grad = key_grad.transpose(0, 2, 1, 3).reshape(TOKENS, KV_HEADS * HD)
    value_grad = value_grad.transpose(0, 2, 1, 3).reshape(TOKENS, KV_HEADS * HD)
    return (attended, query_grad, key_grad, value_grad)
```

```python
import jax
import jax.numpy as jnp
from jax import lax
from jax.sharding import PartitionSpec as P

HD = 128


NEG_FILL = -1e30


def local(queries, keys, values, out_grad, beacon_pos):
    rows = queries.shape[0]
    kv_width = keys.shape[1]
    kv_heads = kv_width // HD
    group_size = queries.shape[1] // HD // kv_heads
    scaling = HD ** (-0.5)
    head_id = lax.axis_index("head")
    shard_id = lax.axis_index("ctx")

    kv_rows = jnp.concatenate([keys, values], axis=1)
    kv_window = lax.all_gather(kv_rows, "head", axis=0, tiled=True)
    window = kv_window.shape[0]
    positions = beacon_pos[0]
    per_shard = positions.shape[0]
    kv_beacons = lax.all_gather(kv_window[positions], "ctx", axis=0, tiled=True)
    beacon_total = kv_beacons.shape[0]
    kv_all = jnp.concatenate([kv_window, kv_beacons], axis=0)
    key_count = window + beacon_total
    key_heads = kv_all[:, :kv_width].reshape(key_count, kv_heads, HD).transpose(1, 0, 2)
    value_heads = kv_all[:, kv_width:].reshape(key_count, kv_heads, HD).transpose(1, 0, 2)

    query_heads = queries.reshape(rows, kv_heads, group_size, HD).transpose(1, 2, 0, 3)
    grad_heads = out_grad.reshape(rows, kv_heads, group_size, HD).transpose(1, 2, 0, 3)

    query_pos = head_id * rows + jnp.arange(rows)
    causal = query_pos[:, None] >= jnp.arange(window)[None, :]
    owners = jnp.arange(beacon_total, dtype=jnp.int32) // per_shard
    seen = jnp.broadcast_to((owners < shard_id)[None, :], (rows, beacon_total))
    visible = jnp.concatenate([causal, seen], axis=1)

    def per_head(inputs):
        q_part, g_part, k_part, v_part = inputs
        scores = jnp.einsum("grd,kd->grk", q_part, k_part, preferred_element_type=jnp.float32) * scaling
        scores = jnp.where(visible, scores, NEG_FILL)
        row_max = jnp.max(scores, axis=-1, keepdims=True)
        weights = jnp.exp(scores - row_max)
        probs = weights / jnp.sum(weights, axis=-1, keepdims=True)
        probs_low = probs.astype(jnp.bfloat16)
        attended = jnp.einsum(
            "grk,kd->grd", probs_low, v_part, preferred_element_type=jnp.float32
        ).astype(jnp.bfloat16)
        row_dot = jnp.sum(
            g_part.astype(jnp.float32) * attended.astype(jnp.float32), axis=-1, keepdims=True
        )
        dprob = jnp.einsum("grd,kd->grk", g_part, v_part, preferred_element_type=jnp.float32)
        grad_scores = (probs * (dprob - row_dot)).astype(jnp.bfloat16)
        query_grad = (
            jnp.einsum("grk,kd->grd", grad_scores, k_part, preferred_element_type=jnp.float32)
            * scaling
        ).astype(jnp.bfloat16)
        key_grad = (
            jnp.einsum("grk,grd->kd", grad_scores, q_part, preferred_element_type=jnp.float32)
            * scaling
        )
        value_grad = jnp.einsum("grk,grd->kd", probs_low, g_part, preferred_element_type=jnp.float32)
        return attended, query_grad, key_grad, value_grad

    attended, query_grad, key_grad, value_grad = lax.map(
        per_head, (query_heads, grad_heads, key_heads, value_heads)
    )
    attended_out = attended.transpose(2, 0, 1, 3).reshape(rows, -1)
    query_out = query_grad.transpose(2, 0, 1, 3).reshape(rows, -1)
    kv_grads = jnp.concatenate(
        [
            key_grad.transpose(1, 0, 2).reshape(key_count, kv_width),
            value_grad.transpose(1, 0, 2).reshape(key_count, kv_width),
        ],
        axis=1,
    )
    own_beacons = lax.psum_scatter(
        kv_grads[window:].astype(jnp.bfloat16), "ctx", scatter_dimension=0, tiled=True
    ).astype(jnp.float32)
    window_grads = kv_grads[:window].at[positions].add(own_beacons)
    own_grads = lax.psum_scatter(
        window_grads.astype(jnp.bfloat16), "head", scatter_dimension=0, tiled=True
    )
    return attended_out, query_out, own_grads[:, :kv_width], own_grads[:, kv_width:]


def solution(mesh):
    in_specs = (
        P(("ctx", "head"), None),
        P(("ctx", "head"), None),
        P(("ctx", "head"), None),
        P(("ctx", "head"), None),
        P("ctx", None),
    )
    out_specs = (
        P(("ctx", "head"), None),
        P(("ctx", "head"), None),
        P(("ctx", "head"), None),
        P(("ctx", "head"), None),
    )
    return jax.shard_map(local, mesh=mesh, in_specs=in_specs, out_specs=out_specs, check_vma=False)
```

```python
import functools
import jax
import jax.numpy as jnp
from jax import lax
from jax.experimental import pallas as pl
from jax.experimental.pallas import tpu as pltpu
from jax.sharding import PartitionSpec as P

HD = 128


NEG_FILL = -1e30


def attention_kernel(
    ids_ref, q_ref, g_ref, k_ref, v_ref, att_ref, dq_ref, dk_ref, dv_ref, *, rows, window, per_shard, group_size
):
    scaling = HD ** (-0.5)
    head_id = ids_ref[0]
    shard_id = ids_ref[1]
    key_count = k_ref.shape[0]
    k = k_ref[...]
    v = v_ref[...]
    row = lax.broadcasted_iota(jnp.int32, (rows, key_count), 0) + head_id * rows
    col = lax.broadcasted_iota(jnp.int32, (rows, key_count), 1)
    in_window = col < window
    visible = (in_window & (row >= col)) | (
        jnp.logical_not(in_window) & (col < window + shard_id * per_shard)
    )
    nt = (((1,), (1,)), ((), ()))
    tn = (((0,), (0,)), ((), ()))
    dk_acc = jnp.zeros((key_count, HD), jnp.float32)
    dv_acc = jnp.zeros((key_count, HD), jnp.float32)
    for g in range(group_size):
        cols = slice(g * HD, (g + 1) * HD)
        q = q_ref[:, cols]
        do = g_ref[:, cols]
        scores = lax.dot_general(q, k, nt, preferred_element_type=jnp.float32) * scaling
        scores = jnp.where(visible, scores, NEG_FILL)
        row_max = jnp.max(scores, axis=1, keepdims=True)
        weights = jnp.exp(scores - row_max)
        probs = weights / jnp.sum(weights, axis=1, keepdims=True)
        probs_low = probs.astype(jnp.bfloat16)
        attended = jnp.dot(probs_low, v, preferred_element_type=jnp.float32).astype(jnp.bfloat16)
        att_ref[:, cols] = attended
        row_dot = jnp.sum(do.astype(jnp.float32) * attended.astype(jnp.float32), axis=1, keepdims=True)
        dprob = lax.dot_general(do, v, nt, preferred_element_type=jnp.float32)
        grad_scores = (probs * (dprob - row_dot)).astype(jnp.bfloat16)
        dq_ref[:, cols] = (
            jnp.dot(grad_scores, k, preferred_element_type=jnp.float32) * scaling
        ).astype(jnp.bfloat16)
        dk_acc = dk_acc + lax.dot_general(grad_scores, q, tn, preferred_element_type=jnp.float32)
        dv_acc = dv_acc + lax.dot_general(probs_low, do, tn, preferred_element_type=jnp.float32)
    dk_ref[...] = dk_acc * scaling
    dv_ref[...] = dv_acc


def attend_all(ids, queries, out_grad, kv_all, window, per_shard):
    rows, q_width = queries.shape
    key_count, kv_double = kv_all.shape
    kv_heads = kv_double // 2 // HD
    group_size = q_width // HD // kv_heads
    kernel = functools.partial(
        attention_kernel, rows=rows, window=window, per_shard=per_shard, group_size=group_size
    )
    qblock = pl.BlockSpec((rows, group_size * HD), lambda h, ids: (0, h))
    kblock = pl.BlockSpec((key_count, HD), lambda h, ids: (0, h))
    vblock = pl.BlockSpec((key_count, HD), lambda h, ids: (0, h + kv_heads))
    return pl.pallas_call(
        kernel,
        grid_spec=pltpu.PrefetchScalarGridSpec(
            num_scalar_prefetch=1,
            grid=(kv_heads,),
            in_specs=[qblock, qblock, kblock, vblock],
            out_specs=[qblock, qblock, kblock, kblock],
        ),
        out_shape=[
            jax.ShapeDtypeStruct((rows, q_width), jnp.bfloat16),
            jax.ShapeDtypeStruct((rows, q_width), jnp.bfloat16),
            jax.ShapeDtypeStruct((key_count, kv_heads * HD), jnp.float32),
            jax.ShapeDtypeStruct((key_count, kv_heads * HD), jnp.float32),
        ],
    )(ids, queries, out_grad, kv_all, kv_all)


def local(queries, keys, values, out_grad, beacon_pos):
    rows = queries.shape[0]
    kv_width = keys.shape[1]
    head_id = lax.axis_index("head")
    shard_id = lax.axis_index("ctx")

    kv_rows = jnp.concatenate([keys, values], axis=1)
    kv_window = lax.all_gather(kv_rows, "head", axis=0, tiled=True)
    window = kv_window.shape[0]
    positions = beacon_pos[0]
    per_shard = positions.shape[0]
    kv_beacons = lax.all_gather(kv_window[positions], "ctx", axis=0, tiled=True)
    kv_all = jnp.concatenate([kv_window, kv_beacons], axis=0)
    ids = jnp.stack([head_id, shard_id]).astype(jnp.int32)
    attended_out, query_out, key_grad, value_grad = attend_all(
        ids, queries, out_grad, kv_all, window, per_shard
    )
    kv_grads = jnp.concatenate([key_grad, value_grad], axis=1)
    own_beacons = lax.psum_scatter(
        kv_grads[window:].astype(jnp.bfloat16), "ctx", scatter_dimension=0, tiled=True
    ).astype(jnp.float32)
    window_grads = kv_grads[:window].at[positions].add(own_beacons)
    own_grads = lax.psum_scatter(
        window_grads.astype(jnp.bfloat16), "head", scatter_dimension=0, tiled=True
    )
    return attended_out, query_out, own_grads[:, :kv_width], own_grads[:, kv_width:]


def solution(mesh):
    in_specs = (
        P(("ctx", "head"), None),
        P(("ctx", "head"), None),
        P(("ctx", "head"), None),
        P(("ctx", "head"), None),
        P("ctx", None),
    )
    out_specs = (
        P(("ctx", "head"), None),
        P(("ctx", "head"), None),
        P(("ctx", "head"), None),
        P(("ctx", "head"), None),
    )
    return jax.shard_map(local, mesh=mesh, in_specs=in_specs, out_specs=out_specs, check_vma=False)
```

```python
import functools
import jax
import jax.numpy as jnp
from jax import lax
from jax.experimental import pallas as pl
from jax.experimental.pallas import tpu as pltpu
from jax.sharding import PartitionSpec as P

HD = 128


NEG_FILL = -1e30


def attention_kernel(
    ids_ref, q_ref, g_ref, k_ref, v_ref, att_ref, dq_ref, dk_ref, dv_ref, *, rows, window, per_shard, group_size
):
    scaling = HD ** (-0.5)
    head_id = ids_ref[0]
    shard_id = ids_ref[1]
    key_count = k_ref.shape[0]
    k = k_ref[...]
    v = v_ref[...]
    row = lax.broadcasted_iota(jnp.int32, (rows, key_count), 0) + head_id * rows
    col = lax.broadcasted_iota(jnp.int32, (rows, key_count), 1)
    in_window = col < window
    visible = (in_window & (row >= col)) | (
        jnp.logical_not(in_window) & (col < window + shard_id * per_shard)
    )
    nt = (((1,), (1,)), ((), ()))
    tn = (((0,), (0,)), ((), ()))
    dk_acc = jnp.zeros((key_count, HD), jnp.float32)
    dv_acc = jnp.zeros((key_count, HD), jnp.float32)
    for g in range(group_size):
        cols = slice(g * HD, (g + 1) * HD)
        q = q_ref[:, cols]
        do = g_ref[:, cols]
        scores = lax.dot_general(q, k, nt, preferred_element_type=jnp.float32) * scaling
        scores = jnp.where(visible, scores, NEG_FILL)
        row_max = jnp.max(scores, axis=1, keepdims=True)
        weights = jnp.exp(scores - row_max)
        probs = weights / jnp.sum(weights, axis=1, keepdims=True)
        probs_low = probs.astype(jnp.bfloat16)
        attended = jnp.dot(probs_low, v, preferred_element_type=jnp.float32).astype(jnp.bfloat16)
        att_ref[:, cols] = attended
        row_dot = jnp.sum(do.astype(jnp.float32) * attended.astype(jnp.float32), axis=1, keepdims=True)
        dprob = lax.dot_general(do, v, nt, preferred_element_type=jnp.float32)
        grad_scores = (probs * (dprob - row_dot)).astype(jnp.bfloat16)
        dq_ref[:, cols] = (
            jnp.dot(grad_scores, k, preferred_element_type=jnp.float32) * scaling
        ).astype(jnp.bfloat16)
        dk_acc = dk_acc + lax.dot_general(grad_scores, q, tn, preferred_element_type=jnp.float32)
        dv_acc = dv_acc + lax.dot_general(probs_low, do, tn, preferred_element_type=jnp.float32)
    dk_ref[...] = dk_acc * scaling
    dv_ref[...] = dv_acc


def attend_all(ids, queries, out_grad, kv_all, window, per_shard):
    rows, q_width = queries.shape
    key_count, kv_double = kv_all.shape
    kv_heads = kv_double // 2 // HD
    group_size = q_width // HD // kv_heads
    kernel = functools.partial(
        attention_kernel, rows=rows, window=window, per_shard=per_shard, group_size=group_size
    )
    qblock = pl.BlockSpec((rows, group_size * HD), lambda h, ids: (0, h))
    kblock = pl.BlockSpec((key_count, HD), lambda h, ids: (0, h))
    vblock = pl.BlockSpec((key_count, HD), lambda h, ids: (0, h + kv_heads))
    return pl.pallas_call(
        kernel,
        grid_spec=pltpu.PrefetchScalarGridSpec(
            num_scalar_prefetch=1,
            grid=(kv_heads,),
            in_specs=[qblock, qblock, kblock, vblock],
            out_specs=[qblock, qblock, kblock, kblock],
        ),
        out_shape=[
            jax.ShapeDtypeStruct((rows, q_width), jnp.bfloat16),
            jax.ShapeDtypeStruct((rows, q_width), jnp.bfloat16),
            jax.ShapeDtypeStruct((key_count, kv_heads * HD), jnp.float32),
            jax.ShapeDtypeStruct((key_count, kv_heads * HD), jnp.float32),
        ],
    )(ids, queries, out_grad, kv_all, kv_all)


def head_gather(block, axis, count):
    index = lax.axis_index(axis)
    from_left, from_right = [block], [block]
    for step in range(1, count):
        from_left.append(
            lax.ppermute(from_left[-1], axis, [(j, j + 1) for j in range(step - 1, count - 1)])
        )
        from_right.append(
            lax.ppermute(from_right[-1], axis, [(j + 1, j) for j in range(count - step)])
        )
    pieces = jnp.stack(from_left + from_right[1:])
    order = jnp.arange(count)
    pick = jnp.where(order <= index, index - order, count - 1 + order - index)
    return pieces[pick].reshape((count * block.shape[0],) + block.shape[1:])


def head_reduce(partials, axis, count):
    index = lax.axis_index(axis)
    rows = partials.shape[0] // count

    def block_of(target):
        return lax.dynamic_slice_in_dim(partials, jnp.clip(target, 0, count - 1) * rows, rows, 0)

    left = jnp.zeros((rows, partials.shape[1]), jnp.bfloat16)
    right = jnp.zeros((rows, partials.shape[1]), jnp.bfloat16)
    for step in range(1, count):
        send_left = (block_of(index + step - count) + left.astype(jnp.float32)).astype(jnp.bfloat16)
        send_right = (block_of(index - step + count) + right.astype(jnp.float32)).astype(jnp.bfloat16)
        left = lax.ppermute(send_left, axis, [(j, j - 1) for j in range(max(1, count - step), count)])
        right = lax.ppermute(send_right, axis, [(j, j + 1) for j in range(0, min(step, count - 1))])
    return block_of(index) + left.astype(jnp.float32) + right.astype(jnp.float32)


def local(queries, keys, values, out_grad, beacon_pos, *, heads_axis, ctx_axis):
    rows = queries.shape[0]
    kv_width = keys.shape[1]
    head_id = lax.axis_index("head")
    shard_id = lax.axis_index("ctx")

    kv_rows = jnp.concatenate([keys, values], axis=1)
    kv_window = head_gather(kv_rows, "head", heads_axis)
    window = kv_window.shape[0]
    positions = beacon_pos[0]
    per_shard = positions.shape[0]
    own_beacon_rows = kv_window[positions]
    kv_beacons = lax.all_to_all(
        jnp.broadcast_to(own_beacon_rows[None], (ctx_axis,) + own_beacon_rows.shape),
        "ctx", 0, 0, tiled=True,
    ).reshape(ctx_axis * per_shard, 2 * kv_width)
    kv_all = jnp.concatenate([kv_window, kv_beacons], axis=0)
    ids = jnp.stack([head_id, shard_id]).astype(jnp.int32)
    attended_out, query_out, key_grad, value_grad = attend_all(
        ids, queries, out_grad, kv_all, window, per_shard
    )
    kv_grads = jnp.concatenate([key_grad, value_grad], axis=1)
    beacon_parts = lax.all_to_all(
        kv_grads[window:].astype(jnp.bfloat16).reshape(ctx_axis, per_shard, 2 * kv_width),
        "ctx", 0, 0, tiled=True,
    )
    own_beacons = jnp.sum(beacon_parts.astype(jnp.float32), axis=0)
    window_grads = kv_grads[:window].at[positions].add(own_beacons)
    own_grads = head_reduce(window_grads, "head", heads_axis).astype(jnp.bfloat16)
    return attended_out, query_out, own_grads[:, :kv_width], own_grads[:, kv_width:]


def solution(mesh):
    in_specs = (
        P(("ctx", "head"), None),
        P(("ctx", "head"), None),
        P(("ctx", "head"), None),
        P(("ctx", "head"), None),
        P("ctx", None),
    )
    out_specs = (
        P(("ctx", "head"), None),
        P(("ctx", "head"), None),
        P(("ctx", "head"), None),
        P(("ctx", "head"), None),
    )
    body = functools.partial(local, heads_axis=mesh.shape["head"], ctx_axis=mesh.shape["ctx"])
    return jax.shard_map(body, mesh=mesh, in_specs=in_specs, out_specs=out_specs, check_vma=False)
```

```python
import functools
import jax
import jax.numpy as jnp
from jax import lax
from jax.experimental import pallas as pl
from jax.experimental.pallas import tpu as pltpu
from jax.sharding import PartitionSpec as P

HD = 128


NEG_FILL = -1e30


def attention_kernel(
    ids_ref, q_ref, g_ref, k_ref, v_ref, att_ref, dq_ref, dk_ref, dv_ref, *, rows, window, per_shard, group_size
):
    scaling = HD ** (-0.5)
    head_id = ids_ref[0]
    shard_id = ids_ref[1]
    key_count = k_ref.shape[0]
    k = k_ref[...]
    v = v_ref[...]
    row = lax.broadcasted_iota(jnp.int32, (rows, key_count), 0) + head_id * rows
    col = lax.broadcasted_iota(jnp.int32, (rows, key_count), 1)
    in_window = col < window
    visible = (in_window & (row >= col)) | (
        jnp.logical_not(in_window) & (col < window + shard_id * per_shard)
    )
    nt = (((1,), (1,)), ((), ()))
    tn = (((0,), (0,)), ((), ()))
    dk_acc = jnp.zeros((key_count, HD), jnp.float32)
    dv_acc = jnp.zeros((key_count, HD), jnp.float32)
    for g in range(group_size):
        cols = slice(g * HD, (g + 1) * HD)
        q = q_ref[:, cols]
        do = g_ref[:, cols]
        scores = lax.dot_general(q, k, nt, preferred_element_type=jnp.float32) * scaling
        scores = jnp.where(visible, scores, NEG_FILL)
        row_max = jnp.max(scores, axis=1, keepdims=True)
        weights = jnp.exp(scores - row_max)
        probs = weights / jnp.sum(weights, axis=1, keepdims=True)
        probs_low = probs.astype(jnp.bfloat16)
        attended = jnp.dot(probs_low, v, preferred_element_type=jnp.float32).astype(jnp.bfloat16)
        att_ref[:, cols] = attended
        row_dot = jnp.sum(do.astype(jnp.float32) * attended.astype(jnp.float32), axis=1, keepdims=True)
        dprob = lax.dot_general(do, v, nt, preferred_element_type=jnp.float32)
        grad_scores = (probs * (dprob - row_dot)).astype(jnp.bfloat16)
        dq_ref[:, cols] = (
            jnp.dot(grad_scores, k, preferred_element_type=jnp.float32) * scaling
        ).astype(jnp.bfloat16)
        dk_acc = dk_acc + lax.dot_general(grad_scores, q, tn, preferred_element_type=jnp.float32)
        dv_acc = dv_acc + lax.dot_general(probs_low, do, tn, preferred_element_type=jnp.float32)
    dk_ref[...] = dk_acc * scaling
    dv_ref[...] = dv_acc


def attend_all(ids, queries, out_grad, kv_all, window, per_shard):
    rows, q_width = queries.shape
    key_count, kv_double = kv_all.shape
    kv_heads = kv_double // 2 // HD
    group_size = q_width // HD // kv_heads
    kernel = functools.partial(
        attention_kernel, rows=rows, window=window, per_shard=per_shard, group_size=group_size
    )
    qblock = pl.BlockSpec((rows, group_size * HD), lambda h, ids: (0, h))
    kblock = pl.BlockSpec((key_count, HD), lambda h, ids: (0, h))
    vblock = pl.BlockSpec((key_count, HD), lambda h, ids: (0, h + kv_heads))
    return pl.pallas_call(
        kernel,
        grid_spec=pltpu.PrefetchScalarGridSpec(
            num_scalar_prefetch=1,
            grid=(kv_heads,),
            in_specs=[qblock, qblock, kblock, vblock],
            out_specs=[qblock, qblock, kblock, kblock],
        ),
        out_shape=[
            jax.ShapeDtypeStruct((rows, q_width), jnp.bfloat16),
            jax.ShapeDtypeStruct((rows, q_width), jnp.bfloat16),
            jax.ShapeDtypeStruct((key_count, kv_heads * HD), jnp.float32),
            jax.ShapeDtypeStruct((key_count, kv_heads * HD), jnp.float32),
        ],
    )(ids, queries, out_grad, kv_all, kv_all)


def head_gather(block, axis, count):
    index = lax.axis_index(axis)
    from_left, from_right = [block], [block]
    for step in range(1, count):
        from_left.append(
            lax.ppermute(from_left[-1], axis, [(j, j + 1) for j in range(step - 1, count - 1)])
        )
        from_right.append(
            lax.ppermute(from_right[-1], axis, [(j + 1, j) for j in range(count - step)])
        )
    pieces = jnp.stack(from_left + from_right[1:])
    order = jnp.arange(count)
    pick = jnp.where(order <= index, index - order, count - 1 + order - index)
    return pieces[pick].reshape((count * block.shape[0],) + block.shape[1:])


def head_reduce(partials, axis, count):
    index = lax.axis_index(axis)
    rows = partials.shape[0] // count

    def block_of(target):
        return lax.dynamic_slice_in_dim(partials, jnp.clip(target, 0, count - 1) * rows, rows, 0)

    left = jnp.zeros((rows, partials.shape[1]), jnp.bfloat16)
    right = jnp.zeros((rows, partials.shape[1]), jnp.bfloat16)
    for step in range(1, count):
        send_left = (block_of(index + step - count) + left.astype(jnp.float32)).astype(jnp.bfloat16)
        send_right = (block_of(index - step + count) + right.astype(jnp.float32)).astype(jnp.bfloat16)
        left = lax.ppermute(send_left, axis, [(j, j - 1) for j in range(max(1, count - step), count)])
        right = lax.ppermute(send_right, axis, [(j, j + 1) for j in range(0, min(step, count - 1))])
    return block_of(index) + left.astype(jnp.float32) + right.astype(jnp.float32)


def local_part(queries, keys, values, out_grad, positions, ids, heads_axis, ctx_axis):
    kv_width = keys.shape[1]
    per_shard = positions.shape[0]
    kv_rows = jnp.concatenate([keys, values], axis=1)
    kv_window = head_gather(kv_rows, "head", heads_axis)
    window = kv_window.shape[0]
    own_beacon_rows = kv_window[positions]
    kv_beacons = lax.all_to_all(
        jnp.broadcast_to(own_beacon_rows[None], (ctx_axis,) + own_beacon_rows.shape),
        "ctx", 0, 0, tiled=True,
    ).reshape(ctx_axis * per_shard, 2 * kv_width)
    kv_all = jnp.concatenate([kv_window, kv_beacons], axis=0)
    attended_out, query_out, key_grad, value_grad = attend_all(
        ids, queries, out_grad, kv_all, window, per_shard
    )
    kv_grads = jnp.concatenate([key_grad, value_grad], axis=1)
    beacon_parts = lax.all_to_all(
        kv_grads[window:].astype(jnp.bfloat16).reshape(ctx_axis, per_shard, 2 * kv_width),
        "ctx", 0, 0, tiled=True,
    )
    own_beacons = jnp.sum(beacon_parts.astype(jnp.float32), axis=0)
    window_grads = kv_grads[:window].at[positions].add(own_beacons)
    own_grads = head_reduce(window_grads, "head", heads_axis).astype(jnp.bfloat16)
    return attended_out, query_out, own_grads[:, :kv_width], own_grads[:, kv_width:]


def local(queries, keys, values, out_grad, beacon_pos, *, heads_axis, ctx_axis, parts):
    head_id = lax.axis_index("head")
    shard_id = lax.axis_index("ctx")
    ids = jnp.stack([head_id, shard_id]).astype(jnp.int32)
    positions = beacon_pos[0]
    q_cols = queries.shape[1] // parts
    kv_cols = keys.shape[1] // parts
    results = []
    for part in range(parts):
        qs = slice(part * q_cols, (part + 1) * q_cols)
        ks = slice(part * kv_cols, (part + 1) * kv_cols)
        results.append(
            local_part(
                queries[:, qs], keys[:, ks], values[:, ks], out_grad[:, qs],
                positions, ids, heads_axis, ctx_axis,
            )
        )
    return tuple(jnp.concatenate(outs, axis=1) for outs in zip(*results))


def solution(mesh):
    in_specs = (
        P(("ctx", "head"), None),
        P(("ctx", "head"), None),
        P(("ctx", "head"), None),
        P(("ctx", "head"), None),
        P("ctx", None),
    )
    out_specs = (
        P(("ctx", "head"), None),
        P(("ctx", "head"), None),
        P(("ctx", "head"), None),
        P(("ctx", "head"), None),
    )
    body = functools.partial(local, heads_axis=mesh.shape["head"], ctx_axis=mesh.shape["ctx"], parts=2)
    return jax.shard_map(body, mesh=mesh, in_specs=in_specs, out_specs=out_specs, check_vma=False)
```

```python
import functools
import jax
import jax.numpy as jnp
from jax import lax
from jax.experimental import pallas as pl
from jax.experimental.pallas import tpu as pltpu
from jax.sharding import PartitionSpec as P

HD = 128


NEG_FILL = -1e30


def attention_kernel(
    ids_ref, q_ref, g_ref, k_ref, v_ref, att_ref, dq_ref, dk_ref, dv_ref, *, rows, window, per_shard, group_size
):
    scaling = HD ** (-0.5)
    head_id = ids_ref[0]
    shard_id = ids_ref[1]
    key_count = k_ref.shape[0]
    k = k_ref[...]
    v = v_ref[...]
    row = lax.broadcasted_iota(jnp.int32, (rows, key_count), 0) + head_id * rows
    col = lax.broadcasted_iota(jnp.int32, (rows, key_count), 1)
    in_window = col < window
    visible = (in_window & (row >= col)) | (
        jnp.logical_not(in_window) & (col < window + shard_id * per_shard)
    )
    nt = (((1,), (1,)), ((), ()))
    tn = (((0,), (0,)), ((), ()))
    dk_acc = jnp.zeros((key_count, HD), jnp.float32)
    dv_acc = jnp.zeros((key_count, HD), jnp.float32)
    for g in range(group_size):
        cols = slice(g * HD, (g + 1) * HD)
        q = q_ref[:, cols]
        do = g_ref[:, cols]
        scores = lax.dot_general(q, k, nt, preferred_element_type=jnp.float32) * scaling
        scores = jnp.where(visible, scores, NEG_FILL)
        row_max = jnp.max(scores, axis=1, keepdims=True)
        weights = jnp.exp(scores - row_max)
        probs = weights / jnp.sum(weights, axis=1, keepdims=True)
        probs_low = probs.astype(jnp.bfloat16)
        attended = jnp.dot(probs_low, v, preferred_element_type=jnp.float32).astype(jnp.bfloat16)
        att_ref[:, cols] = attended
        row_dot = jnp.sum(do.astype(jnp.float32) * attended.astype(jnp.float32), axis=1, keepdims=True)
        dprob = lax.dot_general(do, v, nt, preferred_element_type=jnp.float32)
        grad_scores = (probs * (dprob - row_dot)).astype(jnp.bfloat16)
        dq_ref[:, cols] = (
            jnp.dot(grad_scores, k, preferred_element_type=jnp.float32) * scaling
        ).astype(jnp.bfloat16)
        dk_acc = dk_acc + lax.dot_general(grad_scores, q, tn, preferred_element_type=jnp.float32)
        dv_acc = dv_acc + lax.dot_general(probs_low, do, tn, preferred_element_type=jnp.float32)
    dk_ref[...] = dk_acc * scaling
    dv_ref[...] = dv_acc


def attend_all(ids, queries, out_grad, kv_all, window, per_shard):
    rows, q_width = queries.shape
    key_count, kv_double = kv_all.shape
    kv_heads = kv_double // 2 // HD
    group_size = q_width // HD // kv_heads
    kernel = functools.partial(
        attention_kernel, rows=rows, window=window, per_shard=per_shard, group_size=group_size
    )
    qblock = pl.BlockSpec((rows, group_size * HD), lambda h, ids: (0, h))
    kblock = pl.BlockSpec((key_count, HD), lambda h, ids: (0, h))
    vblock = pl.BlockSpec((key_count, HD), lambda h, ids: (0, h + kv_heads))
    return pl.pallas_call(
        kernel,
        grid_spec=pltpu.PrefetchScalarGridSpec(
            num_scalar_prefetch=1,
            grid=(kv_heads,),
            in_specs=[qblock, qblock, kblock, vblock],
            out_specs=[qblock, qblock, kblock, kblock],
        ),
        out_shape=[
            jax.ShapeDtypeStruct((rows, q_width), jnp.bfloat16),
            jax.ShapeDtypeStruct((rows, q_width), jnp.bfloat16),
            jax.ShapeDtypeStruct((key_count, kv_heads * HD), jnp.float32),
            jax.ShapeDtypeStruct((key_count, kv_heads * HD), jnp.float32),
        ],
    )(ids, queries, out_grad, kv_all, kv_all)


def head_gather(block, axis, count):
    index = lax.axis_index(axis)
    from_left, from_right = [block], [block]
    for step in range(1, count):
        from_left.append(
            lax.ppermute(from_left[-1], axis, [(j, j + 1) for j in range(step - 1, count - 1)])
        )
        from_right.append(
            lax.ppermute(from_right[-1], axis, [(j + 1, j) for j in range(count - step)])
        )
    pieces = jnp.stack(from_left + from_right[1:])
    order = jnp.arange(count)
    pick = jnp.where(order <= index, index - order, count - 1 + order - index)
    return pieces[pick].reshape((count * block.shape[0],) + block.shape[1:])


def head_reduce(partials, axis, count):
    index = lax.axis_index(axis)
    rows = partials.shape[0] // count

    def block_of(target):
        return lax.dynamic_slice_in_dim(partials, jnp.clip(target, 0, count - 1) * rows, rows, 0)

    left = jnp.zeros((rows, partials.shape[1]), jnp.bfloat16)
    right = jnp.zeros((rows, partials.shape[1]), jnp.bfloat16)
    for step in range(1, count):
        send_left = (block_of(index + step - count) + left.astype(jnp.float32)).astype(jnp.bfloat16)
        send_right = (block_of(index - step + count) + right.astype(jnp.float32)).astype(jnp.bfloat16)
        left = lax.ppermute(send_left, axis, [(j, j - 1) for j in range(max(1, count - step), count)])
        right = lax.ppermute(send_right, axis, [(j, j + 1) for j in range(0, min(step, count - 1))])
    return block_of(index) + left.astype(jnp.float32) + right.astype(jnp.float32)


def local_part(queries, keys, values, out_grad, positions, ids, heads_axis, ctx_axis):
    kv_width = keys.shape[1]
    per_shard = positions.shape[0]
    kv_rows = jnp.concatenate([keys, values], axis=1)
    kv_window = head_gather(kv_rows, "head", heads_axis)
    window = kv_window.shape[0]
    own_beacon_rows = kv_window[positions]
    kv_beacons = lax.all_to_all(
        jnp.broadcast_to(own_beacon_rows[None], (ctx_axis,) + own_beacon_rows.shape),
        "ctx", 0, 0, tiled=True,
    ).reshape(ctx_axis * per_shard, 2 * kv_width)
    kv_all = jnp.concatenate([kv_window, kv_beacons], axis=0)
    attended_out, query_out, key_grad, value_grad = attend_all(
        ids, queries, out_grad, kv_all, window, per_shard
    )
    kv_grads = jnp.concatenate([key_grad, value_grad], axis=1)
    beacon_parts = lax.all_to_all(
        kv_grads[window:].astype(jnp.bfloat16).reshape(ctx_axis, per_shard, 2 * kv_width),
        "ctx", 0, 0, tiled=True,
    )
    own_beacons = jnp.sum(beacon_parts.astype(jnp.float32), axis=0)
    window_grads = kv_grads[:window].at[positions].add(own_beacons)
    own_grads = head_reduce(window_grads, "head", heads_axis).astype(jnp.bfloat16)
    return attended_out, query_out, own_grads[:, :kv_width], own_grads[:, kv_width:]


def local(queries, keys, values, out_grad, beacon_pos, *, heads_axis, ctx_axis, parts):
    head_id = lax.axis_index("head")
    shard_id = lax.axis_index("ctx")
    ids = jnp.stack([head_id, shard_id]).astype(jnp.int32)
    positions = beacon_pos[0]
    q_cols = queries.shape[1] // parts
    kv_cols = keys.shape[1] // parts
    results = []
    for part in range(parts):
        qs = slice(part * q_cols, (part + 1) * q_cols)
        ks = slice(part * kv_cols, (part + 1) * kv_cols)
        results.append(
            local_part(
                queries[:, qs], keys[:, ks], values[:, ks], out_grad[:, qs],
                positions, ids, heads_axis, ctx_axis,
            )
        )
    return tuple(jnp.concatenate(outs, axis=1) for outs in zip(*results))


def solution(mesh):
    in_specs = (
        P(("ctx", "head"), None),
        P(("ctx", "head"), None),
        P(("ctx", "head"), None),
        P(("ctx", "head"), None),
        P("ctx", None),
    )
    out_specs = (
        P(("ctx", "head"), None),
        P(("ctx", "head"), None),
        P(("ctx", "head"), None),
        P(("ctx", "head"), None),
    )
    body = functools.partial(local, heads_axis=mesh.shape["head"], ctx_axis=mesh.shape["ctx"], parts=4)
    return jax.shard_map(body, mesh=mesh, in_specs=in_specs, out_specs=out_specs, check_vma=False)
```

```python
import functools
import jax
import jax.numpy as jnp
from jax import lax
from jax.experimental import pallas as pl
from jax.experimental.pallas import tpu as pltpu
from jax.sharding import PartitionSpec as P

HD = 128


NEG_FILL = -1e30


def attention_kernel(
    ids_ref, q_ref, g_ref, k_ref, v_ref, att_ref, dq_ref, dk_ref, dv_ref, *, rows, window, per_shard, group_size
):
    scaling = HD ** (-0.5)
    head_id = ids_ref[0]
    shard_id = ids_ref[1]
    key_count = k_ref.shape[0]
    k = k_ref[...]
    v = v_ref[...]
    row = lax.broadcasted_iota(jnp.int32, (rows, key_count), 0) + head_id * rows
    col = lax.broadcasted_iota(jnp.int32, (rows, key_count), 1)
    in_window = col < window
    visible = (in_window & (row >= col)) | (
        jnp.logical_not(in_window) & (col < window + shard_id * per_shard)
    )
    nt = (((1,), (1,)), ((), ()))
    tn = (((0,), (0,)), ((), ()))
    dk_acc = jnp.zeros((key_count, HD), jnp.float32)
    dv_acc = jnp.zeros((key_count, HD), jnp.float32)
    for g in range(group_size):
        cols = slice(g * HD, (g + 1) * HD)
        q = q_ref[:, cols]
        do = g_ref[:, cols]
        scores = lax.dot_general(q, k, nt, preferred_element_type=jnp.float32) * scaling
        scores = jnp.where(visible, scores, NEG_FILL)
        row_max = jnp.max(scores, axis=1, keepdims=True)
        weights = jnp.exp(scores - row_max)
        probs = weights / jnp.sum(weights, axis=1, keepdims=True)
        probs_low = probs.astype(jnp.bfloat16)
        attended = jnp.dot(probs_low, v, preferred_element_type=jnp.float32).astype(jnp.bfloat16)
        att_ref[:, cols] = attended
        row_dot = jnp.sum(do.astype(jnp.float32) * attended.astype(jnp.float32), axis=1, keepdims=True)
        dprob = lax.dot_general(do, v, nt, preferred_element_type=jnp.float32)
        grad_scores = (probs * (dprob - row_dot)).astype(jnp.bfloat16)
        dq_ref[:, cols] = (
            jnp.dot(grad_scores, k, preferred_element_type=jnp.float32) * scaling
        ).astype(jnp.bfloat16)
        dk_acc = dk_acc + lax.dot_general(grad_scores, q, tn, preferred_element_type=jnp.float32)
        dv_acc = dv_acc + lax.dot_general(probs_low, do, tn, preferred_element_type=jnp.float32)
    dk_ref[...] = dk_acc * scaling
    dv_ref[...] = dv_acc


def attend_all(ids, queries, out_grad, kv_all, window, per_shard):
    rows, q_width = queries.shape
    key_count, kv_double = kv_all.shape
    kv_heads = kv_double // 2 // HD
    group_size = q_width // HD // kv_heads
    kernel = functools.partial(
        attention_kernel, rows=rows, window=window, per_shard=per_shard, group_size=group_size
    )
    qblock = pl.BlockSpec((rows, group_size * HD), lambda h, ids: (0, h))
    kblock = pl.BlockSpec((key_count, HD), lambda h, ids: (0, h))
    vblock = pl.BlockSpec((key_count, HD), lambda h, ids: (0, h + kv_heads))
    return pl.pallas_call(
        kernel,
        grid_spec=pltpu.PrefetchScalarGridSpec(
            num_scalar_prefetch=1,
            grid=(kv_heads,),
            in_specs=[qblock, qblock, kblock, vblock],
            out_specs=[qblock, qblock, kblock, kblock],
        ),
        out_shape=[
            jax.ShapeDtypeStruct((rows, q_width), jnp.bfloat16),
            jax.ShapeDtypeStruct((rows, q_width), jnp.bfloat16),
            jax.ShapeDtypeStruct((key_count, kv_heads * HD), jnp.float32),
            jax.ShapeDtypeStruct((key_count, kv_heads * HD), jnp.float32),
        ],
    )(ids, queries, out_grad, kv_all, kv_all)


def head_gather(block, axis, count):
    index = lax.axis_index(axis)
    from_left, from_right = [block], [block]
    for shift in range(1, count):
        from_left.append(lax.ppermute(block, axis, [(j, j + shift) for j in range(count - shift)]))
        from_right.append(lax.ppermute(block, axis, [(j + shift, j) for j in range(count - shift)]))
    pieces = jnp.stack(from_left + from_right[1:])
    order = jnp.arange(count)
    pick = jnp.where(order <= index, index - order, count - 1 + order - index)
    return pieces[pick].reshape((count * block.shape[0],) + block.shape[1:])


def head_reduce(partials, axis, count):
    index = lax.axis_index(axis)
    rows = partials.shape[0] // count

    def block_of(target):
        return lax.dynamic_slice_in_dim(partials, jnp.clip(target, 0, count - 1) * rows, rows, 0)

    total = block_of(index)
    for shift in range(1, count):
        to_left = block_of(index - shift).astype(jnp.bfloat16)
        to_right = block_of(index + shift).astype(jnp.bfloat16)
        total = total + lax.ppermute(to_left, axis, [(j + shift, j) for j in range(count - shift)]).astype(jnp.float32)
        total = total + lax.ppermute(to_right, axis, [(j, j + shift) for j in range(count - shift)]).astype(jnp.float32)
    return total


def gather_part(keys, values, positions, heads_axis, ctx_axis):
    kv_width = keys.shape[1]
    per_shard = positions.shape[0]
    kv_rows = jnp.concatenate([keys, values], axis=1)
    kv_window = head_gather(kv_rows, "head", heads_axis)
    own_beacon_rows = kv_window[positions]
    kv_beacons = lax.all_to_all(
        jnp.broadcast_to(own_beacon_rows[None], (ctx_axis,) + own_beacon_rows.shape),
        "ctx", 0, 0, tiled=True,
    ).reshape(ctx_axis * per_shard, 2 * kv_width)
    return kv_window, kv_beacons


def grads_part(queries, out_grad, kv_window, kv_beacons, positions, ids, ctx_axis):
    window = kv_window.shape[0]
    per_shard = positions.shape[0]
    kv_all = jnp.concatenate([kv_window, kv_beacons], axis=0)
    attended_out, query_out, key_grad, value_grad = attend_all(
        ids, queries, out_grad, kv_all, window, per_shard
    )
    kv_grads = jnp.concatenate([key_grad, value_grad], axis=1)
    beacon_parts = lax.all_to_all(
        kv_grads[window:].astype(jnp.bfloat16).reshape(ctx_axis, per_shard, kv_grads.shape[1]),
        "ctx", 0, 0, tiled=True,
    )
    own_beacons = jnp.sum(beacon_parts.astype(jnp.float32), axis=0)
    window_grads = kv_grads[:window].at[positions].add(own_beacons)
    return attended_out, query_out, window_grads


def local(queries, keys, values, out_grad, beacon_pos, *, heads_axis, ctx_axis, parts):
    head_id = lax.axis_index("head")
    shard_id = lax.axis_index("ctx")
    ids = jnp.stack([head_id, shard_id]).astype(jnp.int32)
    positions = beacon_pos[0]
    q_cols = queries.shape[1] // parts
    kv_cols = keys.shape[1] // parts
    gathered = []
    ready = None
    for part in range(parts):
        ks = slice(part * kv_cols, (part + 1) * kv_cols)
        part_keys, part_values = keys[:, ks], values[:, ks]
        if ready is not None:
            ready, part_keys, part_values = lax.optimization_barrier((ready, part_keys, part_values))
        gathered.append(gather_part(part_keys, part_values, positions, heads_axis, ctx_axis))
        ready = gathered[-1][0]
    attended, query_grad, key_grad, value_grad = [], [], [], []
    previous = None
    for part in range(parts):
        qs = slice(part * q_cols, (part + 1) * q_cols)
        kv_window, kv_beacons = gathered[part]
        if previous is not None:
            previous, kv_window = lax.optimization_barrier((previous, kv_window))
        attended_out, query_out, window_grads = grads_part(
            queries[:, qs], out_grad[:, qs], kv_window, kv_beacons, positions, ids, ctx_axis
        )
        if previous is not None:
            own = head_reduce(previous, "head", heads_axis).astype(jnp.bfloat16)
            key_grad.append(own[:, :kv_cols])
            value_grad.append(own[:, kv_cols:])
        previous = window_grads
        attended.append(attended_out)
        query_grad.append(query_out)
    own = head_reduce(previous, "head", heads_axis).astype(jnp.bfloat16)
    key_grad.append(own[:, :kv_cols])
    value_grad.append(own[:, kv_cols:])
    return tuple(jnp.concatenate(outs, axis=1) for outs in (attended, query_grad, key_grad, value_grad))


def solution(mesh):
    in_specs = (
        P(("ctx", "head"), None),
        P(("ctx", "head"), None),
        P(("ctx", "head"), None),
        P(("ctx", "head"), None),
        P("ctx", None),
    )
    out_specs = (
        P(("ctx", "head"), None),
        P(("ctx", "head"), None),
        P(("ctx", "head"), None),
        P(("ctx", "head"), None),
    )
    body = functools.partial(local, heads_axis=mesh.shape["head"], ctx_axis=mesh.shape["ctx"], parts=2)
    return jax.shard_map(body, mesh=mesh, in_specs=in_specs, out_specs=out_specs, check_vma=False)
```

```python
import functools
import jax
import jax.numpy as jnp
from jax import lax
from jax.experimental import pallas as pl
from jax.experimental.pallas import tpu as pltpu
from jax.sharding import PartitionSpec as P

HD = 128


NEG_FILL = -1e30


def attention_kernel(
    ids_ref, q_ref, g_ref, k_ref, v_ref, att_ref, dq_ref, dk_ref, dv_ref, *, rows, window, per_shard, group_size
):
    scaling = HD ** (-0.5)
    head_id = ids_ref[0]
    shard_id = ids_ref[1]
    key_count = k_ref.shape[0]
    k = k_ref[...]
    v = v_ref[...]
    row = lax.broadcasted_iota(jnp.int32, (rows, key_count), 0) + head_id * rows
    col = lax.broadcasted_iota(jnp.int32, (rows, key_count), 1)
    in_window = col < window
    visible = (in_window & (row >= col)) | (
        jnp.logical_not(in_window) & (col < window + shard_id * per_shard)
    )
    nt = (((1,), (1,)), ((), ()))
    tn = (((0,), (0,)), ((), ()))
    dk_acc = jnp.zeros((key_count, HD), jnp.float32)
    dv_acc = jnp.zeros((key_count, HD), jnp.float32)
    for g in range(group_size):
        cols = slice(g * HD, (g + 1) * HD)
        q = q_ref[:, cols]
        do = g_ref[:, cols]
        scores = lax.dot_general(q, k, nt, preferred_element_type=jnp.float32) * scaling
        scores = jnp.where(visible, scores, NEG_FILL)
        row_max = jnp.max(scores, axis=1, keepdims=True)
        weights = jnp.exp(scores - row_max)
        probs = weights / jnp.sum(weights, axis=1, keepdims=True)
        probs_low = probs.astype(jnp.bfloat16)
        attended = jnp.dot(probs_low, v, preferred_element_type=jnp.float32).astype(jnp.bfloat16)
        att_ref[:, cols] = attended
        row_dot = jnp.sum(do.astype(jnp.float32) * attended.astype(jnp.float32), axis=1, keepdims=True)
        dprob = lax.dot_general(do, v, nt, preferred_element_type=jnp.float32)
        grad_scores = (probs * (dprob - row_dot)).astype(jnp.bfloat16)
        dq_ref[:, cols] = (
            jnp.dot(grad_scores, k, preferred_element_type=jnp.float32) * scaling
        ).astype(jnp.bfloat16)
        dk_acc = dk_acc + lax.dot_general(grad_scores, q, tn, preferred_element_type=jnp.float32)
        dv_acc = dv_acc + lax.dot_general(probs_low, do, tn, preferred_element_type=jnp.float32)
    dk_ref[...] = dk_acc * scaling
    dv_ref[...] = dv_acc


def attend_all(ids, queries, out_grad, kv_all, window, per_shard):
    rows, q_width = queries.shape
    key_count, kv_double = kv_all.shape
    kv_heads = kv_double // 2 // HD
    group_size = q_width // HD // kv_heads
    kernel = functools.partial(
        attention_kernel, rows=rows, window=window, per_shard=per_shard, group_size=group_size
    )
    qblock = pl.BlockSpec((rows, group_size * HD), lambda h, ids: (0, h))
    kblock = pl.BlockSpec((key_count, HD), lambda h, ids: (0, h))
    vblock = pl.BlockSpec((key_count, HD), lambda h, ids: (0, h + kv_heads))
    return pl.pallas_call(
        kernel,
        grid_spec=pltpu.PrefetchScalarGridSpec(
            num_scalar_prefetch=1,
            grid=(kv_heads,),
            in_specs=[qblock, qblock, kblock, vblock],
            out_specs=[qblock, qblock, kblock, kblock],
        ),
        out_shape=[
            jax.ShapeDtypeStruct((rows, q_width), jnp.bfloat16),
            jax.ShapeDtypeStruct((rows, q_width), jnp.bfloat16),
            jax.ShapeDtypeStruct((key_count, kv_heads * HD), jnp.float32),
            jax.ShapeDtypeStruct((key_count, kv_heads * HD), jnp.float32),
        ],
    )(ids, queries, out_grad, kv_all, kv_all)


def head_gather(block, axis, count):
    index = lax.axis_index(axis)
    from_left, from_right = [block], [block]
    for step in range(1, count):
        from_left.append(
            lax.ppermute(from_left[-1], axis, [(j, j + 1) for j in range(step - 1, count - 1)])
        )
        from_right.append(
            lax.ppermute(from_right[-1], axis, [(j + 1, j) for j in range(count - step)])
        )
    pieces = jnp.stack(from_left + from_right[1:])
    order = jnp.arange(count)
    pick = jnp.where(order <= index, index - order, count - 1 + order - index)
    return pieces[pick].reshape((count * block.shape[0],) + block.shape[1:])


def head_reduce(partials, axis, count):
    rows = partials.shape[0] // count
    received = lax.all_to_all(
        partials.astype(jnp.bfloat16).reshape(count, rows, partials.shape[1]), axis, 0, 0, tiled=True
    )
    return jnp.sum(received.astype(jnp.float32), axis=0)


def local_part(queries, keys, values, out_grad, positions, ids, heads_axis, ctx_axis):
    kv_width = keys.shape[1]
    per_shard = positions.shape[0]
    kv_rows = jnp.concatenate([keys, values], axis=1)
    kv_window = head_gather(kv_rows, "head", heads_axis)
    window = kv_window.shape[0]
    own_beacon_rows = kv_window[positions]
    kv_beacons = lax.all_to_all(
        jnp.broadcast_to(own_beacon_rows[None], (ctx_axis,) + own_beacon_rows.shape),
        "ctx", 0, 0, tiled=True,
    ).reshape(ctx_axis * per_shard, 2 * kv_width)
    kv_all = jnp.concatenate([kv_window, kv_beacons], axis=0)
    attended_out, query_out, key_grad, value_grad = attend_all(
        ids, queries, out_grad, kv_all, window, per_shard
    )
    kv_grads = jnp.concatenate([key_grad, value_grad], axis=1)
    beacon_parts = lax.all_to_all(
        kv_grads[window:].astype(jnp.bfloat16).reshape(ctx_axis, per_shard, 2 * kv_width),
        "ctx", 0, 0, tiled=True,
    )
    own_beacons = jnp.sum(beacon_parts.astype(jnp.float32), axis=0)
    window_grads = kv_grads[:window].at[positions].add(own_beacons)
    own_grads = head_reduce(window_grads, "head", heads_axis).astype(jnp.bfloat16)
    return attended_out, query_out, own_grads[:, :kv_width], own_grads[:, kv_width:]


def local(queries, keys, values, out_grad, beacon_pos, *, heads_axis, ctx_axis, parts):
    head_id = lax.axis_index("head")
    shard_id = lax.axis_index("ctx")
    ids = jnp.stack([head_id, shard_id]).astype(jnp.int32)
    positions = beacon_pos[0]
    q_cols = queries.shape[1] // parts
    kv_cols = keys.shape[1] // parts
    results = []
    for part in range(parts):
        qs = slice(part * q_cols, (part + 1) * q_cols)
        ks = slice(part * kv_cols, (part + 1) * kv_cols)
        results.append(
            local_part(
                queries[:, qs], keys[:, ks], values[:, ks], out_grad[:, qs],
                positions, ids, heads_axis, ctx_axis,
            )
        )
    return tuple(jnp.concatenate(outs, axis=1) for outs in zip(*results))


def solution(mesh):
    in_specs = (
        P(("ctx", "head"), None),
        P(("ctx", "head"), None),
        P(("ctx", "head"), None),
        P(("ctx", "head"), None),
        P("ctx", None),
    )
    out_specs = (
        P(("ctx", "head"), None),
        P(("ctx", "head"), None),
        P(("ctx", "head"), None),
        P(("ctx", "head"), None),
    )
    body = functools.partial(local, heads_axis=mesh.shape["head"], ctx_axis=mesh.shape["ctx"], parts=2)
    return jax.shard_map(body, mesh=mesh, in_specs=in_specs, out_specs=out_specs, check_vma=False)
```

```python
import functools
import jax
import jax.numpy as jnp
from jax import lax
from jax.experimental import pallas as pl
from jax.experimental.pallas import tpu as pltpu
from jax.sharding import PartitionSpec as P

HD = 128


NEG_FILL = -1e30


def attention_kernel(
    ids_ref, q_ref, g_ref, kw_ref, vw_ref, kb_ref, vb_ref, wgrad_ref, bgrad_ref,
    att_ref, dq_ref, *, rows, window, per_shard, group_size
):
    scaling = HD ** (-0.5)
    head_id = ids_ref[0]
    shard_id = ids_ref[1]
    k = jnp.concatenate([kw_ref[...], kb_ref[...]], axis=0)
    v = jnp.concatenate([vw_ref[...], vb_ref[...]], axis=0)
    key_count = k.shape[0]
    row = lax.broadcasted_iota(jnp.int32, (rows, key_count), 0) + head_id * rows
    col = lax.broadcasted_iota(jnp.int32, (rows, key_count), 1)
    in_window = col < window
    visible = (in_window & (row >= col)) | (
        jnp.logical_not(in_window) & (col < window + shard_id * per_shard)
    )
    nt = (((1,), (1,)), ((), ()))
    tn = (((0,), (0,)), ((), ()))
    dk_acc = jnp.zeros((key_count, HD), jnp.float32)
    dv_acc = jnp.zeros((key_count, HD), jnp.float32)
    for g in range(group_size):
        cols = slice(g * HD, (g + 1) * HD)
        q = q_ref[:, cols]
        do = g_ref[:, cols]
        scores = lax.dot_general(q, k, nt, preferred_element_type=jnp.float32) * scaling
        scores = jnp.where(visible, scores, NEG_FILL)
        row_max = jnp.max(scores, axis=1, keepdims=True)
        weights = jnp.exp(scores - row_max)
        probs = weights * (1.0 / jnp.sum(weights, axis=1, keepdims=True))
        probs_low = probs.astype(jnp.bfloat16)
        attended = jnp.dot(probs_low, v, preferred_element_type=jnp.float32).astype(jnp.bfloat16)
        att_ref[:, cols] = attended
        row_dot = jnp.sum(do.astype(jnp.float32) * attended.astype(jnp.float32), axis=1, keepdims=True)
        dprob = lax.dot_general(do, v, nt, preferred_element_type=jnp.float32)
        grad_scores = (probs * (dprob - row_dot)).astype(jnp.bfloat16)
        dq_ref[:, cols] = (
            jnp.dot(grad_scores, k, preferred_element_type=jnp.float32) * scaling
        ).astype(jnp.bfloat16)
        dk_acc = dk_acc + lax.dot_general(grad_scores, q, tn, preferred_element_type=jnp.float32)
        dv_acc = dv_acc + lax.dot_general(probs_low, do, tn, preferred_element_type=jnp.float32)
    dk_acc = dk_acc * scaling
    wgrad_ref[:, :HD] = dk_acc[:window]
    wgrad_ref[:, HD:] = dv_acc[:window]
    bgrad_ref[:, :HD] = dk_acc[window:].astype(jnp.bfloat16)
    bgrad_ref[:, HD:] = dv_acc[window:].astype(jnp.bfloat16)


def attend_all(ids, queries, out_grad, kv_window, kv_beacons, per_shard):
    rows, q_width = queries.shape
    window, kv_double = kv_window.shape
    beacon_total = kv_beacons.shape[0]
    kv_heads = kv_double // 2 // HD
    group_size = q_width // HD // kv_heads
    kernel = functools.partial(
        attention_kernel, rows=rows, window=window, per_shard=per_shard, group_size=group_size
    )
    qblock = pl.BlockSpec((rows, group_size * HD), lambda h, ids: (0, h))
    kwblock = pl.BlockSpec((window, HD), lambda h, ids: (0, h))
    vwblock = pl.BlockSpec((window, HD), lambda h, ids: (0, h + kv_heads))
    kbblock = pl.BlockSpec((beacon_total, HD), lambda h, ids: (0, h))
    vbblock = pl.BlockSpec((beacon_total, HD), lambda h, ids: (0, h + kv_heads))
    wgblock = pl.BlockSpec((window, 2 * HD), lambda h, ids: (0, h))
    bgblock = pl.BlockSpec((beacon_total, 2 * HD), lambda h, ids: (0, h))
    return pl.pallas_call(
        kernel,
        grid_spec=pltpu.PrefetchScalarGridSpec(
            num_scalar_prefetch=1,
            grid=(kv_heads,),
            in_specs=[qblock, qblock, kwblock, vwblock, kbblock, vbblock],
            out_specs=[wgblock, bgblock, qblock, qblock],
        ),
        out_shape=[
            jax.ShapeDtypeStruct((window, kv_double), jnp.float32),
            jax.ShapeDtypeStruct((beacon_total, kv_double), jnp.bfloat16),
            jax.ShapeDtypeStruct((rows, q_width), jnp.bfloat16),
            jax.ShapeDtypeStruct((rows, q_width), jnp.bfloat16),
        ],
    )(ids, queries, out_grad, kv_window, kv_window, kv_beacons, kv_beacons)


def head_gather(block, axis, count):
    index = lax.axis_index(axis)
    from_left, from_right = [block], [block]
    for step in range(1, count):
        from_left.append(
            lax.ppermute(from_left[-1], axis, [(j, j + 1) for j in range(step - 1, count - 1)])
        )
        from_right.append(
            lax.ppermute(from_right[-1], axis, [(j + 1, j) for j in range(count - step)])
        )
    pieces = jnp.stack(from_left + from_right[1:])
    order = jnp.arange(count)
    pick = jnp.where(order <= index, index - order, count - 1 + order - index)
    return pieces[pick].reshape((count * block.shape[0],) + block.shape[1:])


def head_reduce(partials, axis, count):
    index = lax.axis_index(axis)
    rows = partials.shape[0] // count

    def block_of(target):
        return lax.dynamic_slice_in_dim(partials, jnp.clip(target, 0, count - 1) * rows, rows, 0)

    left = jnp.zeros((rows, partials.shape[1]), jnp.bfloat16)
    right = jnp.zeros((rows, partials.shape[1]), jnp.bfloat16)
    for step in range(1, count):
        send_left = (block_of(index + step - count) + left.astype(jnp.float32)).astype(jnp.bfloat16)
        send_right = (block_of(index - step + count) + right.astype(jnp.float32)).astype(jnp.bfloat16)
        left = lax.ppermute(send_left, axis, [(j, j - 1) for j in range(max(1, count - step), count)])
        right = lax.ppermute(send_right, axis, [(j, j + 1) for j in range(0, min(step, count - 1))])
    return block_of(index) + left.astype(jnp.float32) + right.astype(jnp.float32)


def local_part(queries, keys, values, out_grad, positions, ids, heads_axis, ctx_axis):
    kv_width = keys.shape[1]
    per_shard = positions.shape[0]
    kv_rows = jnp.concatenate([keys, values], axis=1)
    kv_window = head_gather(kv_rows, "head", heads_axis)
    window = kv_window.shape[0]
    own_beacon_rows = kv_window[positions]
    kv_beacons = lax.all_to_all(
        jnp.broadcast_to(own_beacon_rows[None], (ctx_axis,) + own_beacon_rows.shape),
        "ctx", 0, 0, tiled=True,
    ).reshape(ctx_axis * per_shard, 2 * kv_width)
    window_grads, beacon_grads, attended_out, query_out = attend_all(
        ids, queries, out_grad, kv_window, kv_beacons, per_shard
    )
    beacon_parts = lax.all_to_all(
        beacon_grads.reshape(ctx_axis, per_shard, 2 * kv_width), "ctx", 0, 0, tiled=True
    )
    own_beacons = jnp.sum(beacon_parts.astype(jnp.float32), axis=0)
    window_grads = window_grads.at[positions].add(own_beacons)
    own_grads = head_reduce(window_grads, "head", heads_axis).astype(jnp.bfloat16)
    own_grads = own_grads.reshape(own_grads.shape[0], kv_width // HD, 2, HD)
    rows = own_grads.shape[0]
    return (
        attended_out, query_out,
        own_grads[:, :, 0].reshape(rows, kv_width), own_grads[:, :, 1].reshape(rows, kv_width),
    )


def local(queries, keys, values, out_grad, beacon_pos, *, heads_axis, ctx_axis, parts):
    head_id = lax.axis_index("head")
    shard_id = lax.axis_index("ctx")
    ids = jnp.stack([head_id, shard_id]).astype(jnp.int32)
    positions = beacon_pos[0]
    q_cols = queries.shape[1] // parts
    kv_cols = keys.shape[1] // parts
    results = []
    for part in range(parts):
        qs = slice(part * q_cols, (part + 1) * q_cols)
        ks = slice(part * kv_cols, (part + 1) * kv_cols)
        results.append(
            local_part(
                queries[:, qs], keys[:, ks], values[:, ks], out_grad[:, qs],
                positions, ids, heads_axis, ctx_axis,
            )
        )
    return tuple(jnp.concatenate(outs, axis=1) for outs in zip(*results))


def solution(mesh):
    in_specs = (
        P(("ctx", "head"), None),
        P(("ctx", "head"), None),
        P(("ctx", "head"), None),
        P(("ctx", "head"), None),
        P("ctx", None),
    )
    out_specs = (
        P(("ctx", "head"), None),
        P(("ctx", "head"), None),
        P(("ctx", "head"), None),
        P(("ctx", "head"), None),
    )
    body = functools.partial(local, heads_axis=mesh.shape["head"], ctx_axis=mesh.shape["ctx"], parts=2)
    return jax.shard_map(body, mesh=mesh, in_specs=in_specs, out_specs=out_specs, check_vma=False)
```

```python
import functools
import jax
import jax.numpy as jnp
from jax import lax
from jax.experimental import pallas as pl
from jax.experimental.pallas import tpu as pltpu
from jax.sharding import PartitionSpec as P

HD = 128


NEG_FILL = -1e30


def attention_kernel(
    ids_ref, q_ref, g_ref, kw_ref, vw_ref, kb_ref, vb_ref, wgrad_ref, bgrad_ref,
    att_ref, dq_ref, *, rows, window, per_shard, group_size
):
    scaling = HD ** (-0.5)
    head_id = ids_ref[0]
    shard_id = ids_ref[1]
    k = jnp.concatenate([kw_ref[...], kb_ref[...]], axis=0)
    v = jnp.concatenate([vw_ref[...], vb_ref[...]], axis=0)
    key_count = k.shape[0]
    stacked = rows * group_size
    row = lax.rem(lax.broadcasted_iota(jnp.int32, (stacked, key_count), 0), rows) + head_id * rows
    col = lax.broadcasted_iota(jnp.int32, (stacked, key_count), 1)
    in_window = col < window
    visible = (in_window & (row >= col)) | (
        jnp.logical_not(in_window) & (col < window + shard_id * per_shard)
    )
    nt = (((1,), (1,)), ((), ()))
    tn = (((0,), (0,)), ((), ()))
    q = jnp.concatenate([q_ref[:, g * HD:(g + 1) * HD] for g in range(group_size)], axis=0)
    do = jnp.concatenate([g_ref[:, g * HD:(g + 1) * HD] for g in range(group_size)], axis=0)
    scores = lax.dot_general(q, k, nt, preferred_element_type=jnp.float32) * scaling
    scores = jnp.where(visible, scores, NEG_FILL)
    row_max = jnp.max(scores, axis=1, keepdims=True)
    weights = jnp.exp(scores - row_max)
    probs = weights / jnp.sum(weights, axis=1, keepdims=True)
    probs_low = probs.astype(jnp.bfloat16)
    attended = jnp.dot(probs_low, v, preferred_element_type=jnp.float32).astype(jnp.bfloat16)
    row_dot = jnp.sum(do.astype(jnp.float32) * attended.astype(jnp.float32), axis=1, keepdims=True)
    dprob = lax.dot_general(do, v, nt, preferred_element_type=jnp.float32)
    grad_scores = (probs * (dprob - row_dot)).astype(jnp.bfloat16)
    query_grad = (
        jnp.dot(grad_scores, k, preferred_element_type=jnp.float32) * scaling
    ).astype(jnp.bfloat16)
    for g in range(group_size):
        att_ref[:, g * HD:(g + 1) * HD] = attended[g * rows:(g + 1) * rows]
        dq_ref[:, g * HD:(g + 1) * HD] = query_grad[g * rows:(g + 1) * rows]
    key_grad = (lax.dot_general(q, grad_scores, tn, preferred_element_type=jnp.float32) * scaling).T
    value_grad = lax.dot_general(do, probs_low, tn, preferred_element_type=jnp.float32).T
    wgrad_ref[:, :HD] = key_grad[:window]
    wgrad_ref[:, HD:] = value_grad[:window]
    bgrad_ref[:, :HD] = key_grad[window:].astype(jnp.bfloat16)
    bgrad_ref[:, HD:] = value_grad[window:].astype(jnp.bfloat16)


def attend_all(ids, queries, out_grad, kv_window, kv_beacons, per_shard):
    rows, q_width = queries.shape
    window, kv_double = kv_window.shape
    beacon_total = kv_beacons.shape[0]
    kv_heads = kv_double // 2 // HD
    group_size = q_width // HD // kv_heads
    kernel = functools.partial(
        attention_kernel, rows=rows, window=window, per_shard=per_shard, group_size=group_size
    )
    qblock = pl.BlockSpec((rows, group_size * HD), lambda h, ids: (0, h))
    kwblock = pl.BlockSpec((window, HD), lambda h, ids: (0, h))
    vwblock = pl.BlockSpec((window, HD), lambda h, ids: (0, h + kv_heads))
    kbblock = pl.BlockSpec((beacon_total, HD), lambda h, ids: (0, h))
    vbblock = pl.BlockSpec((beacon_total, HD), lambda h, ids: (0, h + kv_heads))
    wgblock = pl.BlockSpec((window, 2 * HD), lambda h, ids: (0, h))
    bgblock = pl.BlockSpec((beacon_total, 2 * HD), lambda h, ids: (0, h))
    return pl.pallas_call(
        kernel,
        grid_spec=pltpu.PrefetchScalarGridSpec(
            num_scalar_prefetch=1,
            grid=(kv_heads,),
            in_specs=[qblock, qblock, kwblock, vwblock, kbblock, vbblock],
            out_specs=[wgblock, bgblock, qblock, qblock],
        ),
        out_shape=[
            jax.ShapeDtypeStruct((window, kv_double), jnp.float32),
            jax.ShapeDtypeStruct((beacon_total, kv_double), jnp.bfloat16),
            jax.ShapeDtypeStruct((rows, q_width), jnp.bfloat16),
            jax.ShapeDtypeStruct((rows, q_width), jnp.bfloat16),
        ],
    )(ids, queries, out_grad, kv_window, kv_window, kv_beacons, kv_beacons)


def head_gather(block, axis, count):
    index = lax.axis_index(axis)
    from_left, from_right = [block], [block]
    for step in range(1, count):
        from_left.append(
            lax.ppermute(from_left[-1], axis, [(j, j + 1) for j in range(step - 1, count - 1)])
        )
        from_right.append(
            lax.ppermute(from_right[-1], axis, [(j + 1, j) for j in range(count - step)])
        )
    pieces = jnp.stack(from_left + from_right[1:])
    order = jnp.arange(count)
    pick = jnp.where(order <= index, index - order, count - 1 + order - index)
    return pieces[pick].reshape((count * block.shape[0],) + block.shape[1:])


def head_reduce(partials, axis, count):
    index = lax.axis_index(axis)
    rows = partials.shape[0] // count

    def block_of(target):
        return lax.dynamic_slice_in_dim(partials, jnp.clip(target, 0, count - 1) * rows, rows, 0)

    left = jnp.zeros((rows, partials.shape[1]), jnp.bfloat16)
    right = jnp.zeros((rows, partials.shape[1]), jnp.bfloat16)
    for step in range(1, count):
        send_left = (block_of(index + step - count) + left.astype(jnp.float32)).astype(jnp.bfloat16)
        send_right = (block_of(index - step + count) + right.astype(jnp.float32)).astype(jnp.bfloat16)
        left = lax.ppermute(send_left, axis, [(j, j - 1) for j in range(max(1, count - step), count)])
        right = lax.ppermute(send_right, axis, [(j, j + 1) for j in range(0, min(step, count - 1))])
    return block_of(index) + left.astype(jnp.float32) + right.astype(jnp.float32)


def local_part(queries, keys, values, out_grad, positions, ids, heads_axis, ctx_axis):
    kv_width = keys.shape[1]
    per_shard = positions.shape[0]
    kv_rows = jnp.concatenate([keys, values], axis=1)
    kv_window = head_gather(kv_rows, "head", heads_axis)
    window = kv_window.shape[0]
    own_beacon_rows = kv_window[positions]
    kv_beacons = lax.all_to_all(
        jnp.broadcast_to(own_beacon_rows[None], (ctx_axis,) + own_beacon_rows.shape),
        "ctx", 0, 0, tiled=True,
    ).reshape(ctx_axis * per_shard, 2 * kv_width)
    window_grads, beacon_grads, attended_out, query_out = attend_all(
        ids, queries, out_grad, kv_window, kv_beacons, per_shard
    )
    beacon_parts = lax.all_to_all(
        beacon_grads.reshape(ctx_axis, per_shard, 2 * kv_width), "ctx", 0, 0, tiled=True
    )
    own_beacons = jnp.sum(beacon_parts.astype(jnp.float32), axis=0)
    window_grads = window_grads.at[positions].add(own_beacons)
    own_grads = head_reduce(window_grads, "head", heads_axis).astype(jnp.bfloat16)
    own_grads = own_grads.reshape(own_grads.shape[0], kv_width // HD, 2, HD)
    rows = own_grads.shape[0]
    return (
        attended_out, query_out,
        own_grads[:, :, 0].reshape(rows, kv_width), own_grads[:, :, 1].reshape(rows, kv_width),
    )


def local(queries, keys, values, out_grad, beacon_pos, *, heads_axis, ctx_axis, parts):
    head_id = lax.axis_index("head")
    shard_id = lax.axis_index("ctx")
    ids = jnp.stack([head_id, shard_id]).astype(jnp.int32)
    positions = beacon_pos[0]
    q_cols = queries.shape[1] // parts
    kv_cols = keys.shape[1] // parts
    results = []
    for part in range(parts):
        qs = slice(part * q_cols, (part + 1) * q_cols)
        ks = slice(part * kv_cols, (part + 1) * kv_cols)
        results.append(
            local_part(
                queries[:, qs], keys[:, ks], values[:, ks], out_grad[:, qs],
                positions, ids, heads_axis, ctx_axis,
            )
        )
    return tuple(jnp.concatenate(outs, axis=1) for outs in zip(*results))


def solution(mesh):
    in_specs = (
        P(("ctx", "head"), None),
        P(("ctx", "head"), None),
        P(("ctx", "head"), None),
        P(("ctx", "head"), None),
        P("ctx", None),
    )
    out_specs = (
        P(("ctx", "head"), None),
        P(("ctx", "head"), None),
        P(("ctx", "head"), None),
        P(("ctx", "head"), None),
    )
    body = functools.partial(local, heads_axis=mesh.shape["head"], ctx_axis=mesh.shape["ctx"], parts=2)
    return jax.shard_map(body, mesh=mesh, in_specs=in_specs, out_specs=out_specs, check_vma=False)
```

```python
import functools
import jax
import jax.numpy as jnp
from jax import lax
from jax.experimental import pallas as pl
from jax.experimental.pallas import tpu as pltpu
from jax.sharding import PartitionSpec as P

HD = 128


NEG_FILL = -1e30


def attention_kernel(
    ids_ref, q_ref, g_ref, kw_ref, vw_ref, kb_ref, vb_ref, wgrad_ref, bgrad_ref,
    att_ref, dq_ref, *, rows, window, per_shard, group_size
):
    scaling = HD ** (-0.5)
    head_id = ids_ref[0]
    shard_id = ids_ref[1]
    k = jnp.concatenate([kw_ref[...], kb_ref[...]], axis=0)
    v = jnp.concatenate([vw_ref[...], vb_ref[...]], axis=0)
    key_count = k.shape[0]
    stacked = rows * group_size
    row = lax.rem(lax.broadcasted_iota(jnp.int32, (stacked, key_count), 0), rows) + head_id * rows
    col = lax.broadcasted_iota(jnp.int32, (stacked, key_count), 1)
    in_window = col < window
    visible = (in_window & (row >= col)) | (
        jnp.logical_not(in_window) & (col < window + shard_id * per_shard)
    )
    nt = (((1,), (1,)), ((), ()))
    tn = (((0,), (0,)), ((), ()))
    q = jnp.concatenate([q_ref[:, g * HD:(g + 1) * HD] for g in range(group_size)], axis=0)
    do = jnp.concatenate([g_ref[:, g * HD:(g + 1) * HD] for g in range(group_size)], axis=0)
    scores = lax.dot_general(q, k, nt, preferred_element_type=jnp.float32) * scaling
    scores = jnp.where(visible, scores, NEG_FILL)
    row_max = jnp.max(scores, axis=1, keepdims=True)
    weights = jnp.exp(scores - row_max)
    probs = weights / jnp.sum(weights, axis=1, keepdims=True)
    probs_low = probs.astype(jnp.bfloat16)
    attended = jnp.dot(probs_low, v, preferred_element_type=jnp.float32).astype(jnp.bfloat16)
    row_dot = jnp.sum(do.astype(jnp.float32) * attended.astype(jnp.float32), axis=1, keepdims=True)
    dprob = lax.dot_general(do, v, nt, preferred_element_type=jnp.float32)
    grad_scores = (probs * (dprob - row_dot)).astype(jnp.bfloat16)
    query_grad = (
        jnp.dot(grad_scores, k, preferred_element_type=jnp.float32) * scaling
    ).astype(jnp.bfloat16)
    for g in range(group_size):
        att_ref[:, g * HD:(g + 1) * HD] = attended[g * rows:(g + 1) * rows]
        dq_ref[:, g * HD:(g + 1) * HD] = query_grad[g * rows:(g + 1) * rows]
    key_grad = (lax.dot_general(q, grad_scores, tn, preferred_element_type=jnp.float32) * scaling).T
    value_grad = lax.dot_general(do, probs_low, tn, preferred_element_type=jnp.float32).T
    wgrad_ref[:, :HD] = key_grad[:window]
    wgrad_ref[:, HD:] = value_grad[:window]
    bgrad_ref[:, :HD] = key_grad[window:].astype(jnp.bfloat16)
    bgrad_ref[:, HD:] = value_grad[window:].astype(jnp.bfloat16)


def attend_all(ids, queries, out_grad, kv_window, kv_beacons, per_shard):
    rows, q_width = queries.shape
    window, kv_double = kv_window.shape
    beacon_total = kv_beacons.shape[0]
    kv_heads = kv_double // 2 // HD
    group_size = q_width // HD // kv_heads
    kernel = functools.partial(
        attention_kernel, rows=rows, window=window, per_shard=per_shard, group_size=group_size
    )
    qblock = pl.BlockSpec((rows, group_size * HD), lambda h, ids: (0, h))
    kwblock = pl.BlockSpec((window, HD), lambda h, ids: (0, h))
    vwblock = pl.BlockSpec((window, HD), lambda h, ids: (0, h + kv_heads))
    kbblock = pl.BlockSpec((beacon_total, HD), lambda h, ids: (0, h))
    vbblock = pl.BlockSpec((beacon_total, HD), lambda h, ids: (0, h + kv_heads))
    wgblock = pl.BlockSpec((window, 2 * HD), lambda h, ids: (0, h))
    bgblock = pl.BlockSpec((beacon_total, 2 * HD), lambda h, ids: (0, h))
    return pl.pallas_call(
        kernel,
        grid_spec=pltpu.PrefetchScalarGridSpec(
            num_scalar_prefetch=1,
            grid=(kv_heads,),
            in_specs=[qblock, qblock, kwblock, vwblock, kbblock, vbblock],
            out_specs=[wgblock, bgblock, qblock, qblock],
        ),
        out_shape=[
            jax.ShapeDtypeStruct((window, kv_double), jnp.float32),
            jax.ShapeDtypeStruct((beacon_total, kv_double), jnp.bfloat16),
            jax.ShapeDtypeStruct((rows, q_width), jnp.bfloat16),
            jax.ShapeDtypeStruct((rows, q_width), jnp.bfloat16),
        ],
    )(ids, queries, out_grad, kv_window, kv_window, kv_beacons, kv_beacons)


def head_gather(block, axis, count):
    index = lax.axis_index(axis)
    from_left, from_right = [block], [block]
    for step in range(1, count):
        from_left.append(
            lax.ppermute(from_left[-1], axis, [(j, j + 1) for j in range(step - 1, count - 1)])
        )
        from_right.append(
            lax.ppermute(from_right[-1], axis, [(j + 1, j) for j in range(count - step)])
        )
    pieces = jnp.stack(from_left + from_right[1:])
    order = jnp.arange(count)
    pick = jnp.where(order <= index, index - order, count - 1 + order - index)
    return pieces[pick].reshape((count * block.shape[0],) + block.shape[1:])


def head_reduce(partials, axis, count):
    index = lax.axis_index(axis)
    rows = partials.shape[0] // count

    def block_of(target):
        return lax.dynamic_slice_in_dim(partials, jnp.clip(target, 0, count - 1) * rows, rows, 0)

    left = jnp.zeros((rows, partials.shape[1]), jnp.bfloat16)
    right = jnp.zeros((rows, partials.shape[1]), jnp.bfloat16)
    for step in range(1, count):
        send_left = (block_of(index + step - count) + left.astype(jnp.float32)).astype(jnp.bfloat16)
        send_right = (block_of(index - step + count) + right.astype(jnp.float32)).astype(jnp.bfloat16)
        left = lax.ppermute(send_left, axis, [(j, j - 1) for j in range(max(1, count - step), count)])
        right = lax.ppermute(send_right, axis, [(j, j + 1) for j in range(0, min(step, count - 1))])
    return block_of(index) + left.astype(jnp.float32) + right.astype(jnp.float32)


def local_part(queries, keys, values, out_grad, positions, ids, heads_axis, ctx_axis):
    kv_width = keys.shape[1]
    per_shard = positions.shape[0]
    kv_rows = jnp.concatenate([keys, values], axis=1)
    kv_window = head_gather(kv_rows, "head", heads_axis)
    window = kv_window.shape[0]
    own_beacon_rows = kv_window[positions]
    kv_beacons = lax.all_to_all(
        jnp.broadcast_to(own_beacon_rows[None], (ctx_axis,) + own_beacon_rows.shape),
        "ctx", 0, 0, tiled=True,
    ).reshape(ctx_axis * per_shard, 2 * kv_width)
    window_grads, beacon_grads, attended_out, query_out = attend_all(
        ids, queries, out_grad, kv_window, kv_beacons, per_shard
    )
    beacon_parts = lax.all_to_all(
        beacon_grads.reshape(ctx_axis, per_shard, 2 * kv_width), "ctx", 0, 0, tiled=True
    )
    own_beacons = jnp.sum(beacon_parts.astype(jnp.float32), axis=0)
    window_grads = window_grads.at[positions].add(own_beacons)
    own_grads = head_reduce(window_grads, "head", heads_axis).astype(jnp.bfloat16)
    own_grads = own_grads.reshape(own_grads.shape[0], kv_width // HD, 2, HD)
    rows = own_grads.shape[0]
    return (
        attended_out, query_out,
        own_grads[:, :, 0].reshape(rows, kv_width), own_grads[:, :, 1].reshape(rows, kv_width),
        kv_window,
    )


def local(queries, keys, values, out_grad, beacon_pos, *, heads_axis, ctx_axis, parts):
    head_id = lax.axis_index("head")
    shard_id = lax.axis_index("ctx")
    ids = jnp.stack([head_id, shard_id]).astype(jnp.int32)
    positions = beacon_pos[0]
    q_cols = queries.shape[1] // parts
    kv_cols = keys.shape[1] // parts
    results = []
    ready = None
    for part in range(parts):
        qs = slice(part * q_cols, (part + 1) * q_cols)
        ks = slice(part * kv_cols, (part + 1) * kv_cols)
        part_keys, part_values = keys[:, ks], values[:, ks]
        if ready is not None:
            ready, part_keys, part_values = lax.optimization_barrier((ready, part_keys, part_values))
        results.append(
            local_part(
                queries[:, qs], part_keys, part_values, out_grad[:, qs],
                positions, ids, heads_axis, ctx_axis,
            )
        )
        ready = results[-1][4]
    return tuple(jnp.concatenate(outs, axis=1) for outs in list(zip(*results))[:4])


def solution(mesh):
    in_specs = (
        P(("ctx", "head"), None),
        P(("ctx", "head"), None),
        P(("ctx", "head"), None),
        P(("ctx", "head"), None),
        P("ctx", None),
    )
    out_specs = (
        P(("ctx", "head"), None),
        P(("ctx", "head"), None),
        P(("ctx", "head"), None),
        P(("ctx", "head"), None),
    )
    body = functools.partial(local, heads_axis=mesh.shape["head"], ctx_axis=mesh.shape["ctx"], parts=2)
    return jax.shard_map(body, mesh=mesh, in_specs=in_specs, out_specs=out_specs, check_vma=False)
```

```python
import functools
import jax
import jax.numpy as jnp
from jax import lax
from jax.experimental import pallas as pl
from jax.experimental.pallas import tpu as pltpu
from jax.sharding import PartitionSpec as P

HD = 128


NEG_FILL = -1e30


def attention_kernel(
    ids_ref, q_ref, g_ref, kw_ref, vw_ref, kb_ref, vb_ref, wgrad_ref, bgrad_ref,
    att_ref, dq_ref, *, rows, window, per_shard, group_size
):
    scaling = HD ** (-0.5)
    head_id = ids_ref[0]
    shard_id = ids_ref[1]
    k = jnp.concatenate([kw_ref[...], kb_ref[...]], axis=0)
    v = jnp.concatenate([vw_ref[...], vb_ref[...]], axis=0)
    key_count = k.shape[0]
    stacked = rows * group_size
    row = lax.rem(lax.broadcasted_iota(jnp.int32, (stacked, key_count), 0), rows) + head_id * rows
    col = lax.broadcasted_iota(jnp.int32, (stacked, key_count), 1)
    in_window = col < window
    visible = (in_window & (row >= col)) | (
        jnp.logical_not(in_window) & (col < window + shard_id * per_shard)
    )
    nt = (((1,), (1,)), ((), ()))
    tn = (((0,), (0,)), ((), ()))
    q = jnp.concatenate([q_ref[:, g * HD:(g + 1) * HD] for g in range(group_size)], axis=0)
    do = jnp.concatenate([g_ref[:, g * HD:(g + 1) * HD] for g in range(group_size)], axis=0)
    scores = lax.dot_general(q, k, nt, preferred_element_type=jnp.float32) * scaling
    scores = jnp.where(visible, scores, NEG_FILL)
    row_max = jnp.max(scores, axis=1, keepdims=True)
    weights = jnp.exp(scores - row_max)
    probs = weights / jnp.sum(weights, axis=1, keepdims=True)
    probs_low = probs.astype(jnp.bfloat16)
    attended = jnp.dot(probs_low, v, preferred_element_type=jnp.float32).astype(jnp.bfloat16)
    row_dot = jnp.sum(do.astype(jnp.float32) * attended.astype(jnp.float32), axis=1, keepdims=True)
    dprob = lax.dot_general(do, v, nt, preferred_element_type=jnp.float32)
    grad_scores = (probs * (dprob - row_dot)).astype(jnp.bfloat16)
    query_grad = (
        jnp.dot(grad_scores, k, preferred_element_type=jnp.float32) * scaling
    ).astype(jnp.bfloat16)
    for g in range(group_size):
        att_ref[:, g * HD:(g + 1) * HD] = attended[g * rows:(g + 1) * rows]
        dq_ref[:, g * HD:(g + 1) * HD] = query_grad[g * rows:(g + 1) * rows]
    key_grad = (lax.dot_general(q, grad_scores, tn, preferred_element_type=jnp.float32) * scaling).T
    value_grad = lax.dot_general(do, probs_low, tn, preferred_element_type=jnp.float32).T
    wgrad_ref[:, :HD] = key_grad[:window]
    wgrad_ref[:, HD:] = value_grad[:window]
    bgrad_ref[:, :HD] = key_grad[window:].astype(jnp.bfloat16)
    bgrad_ref[:, HD:] = value_grad[window:].astype(jnp.bfloat16)


def attend_all(ids, queries, out_grad, kv_window, kv_beacons, per_shard):
    rows, q_width = queries.shape
    window, kv_double = kv_window.shape
    beacon_total = kv_beacons.shape[0]
    kv_heads = kv_double // 2 // HD
    group_size = q_width // HD // kv_heads
    kernel = functools.partial(
        attention_kernel, rows=rows, window=window, per_shard=per_shard, group_size=group_size
    )
    qblock = pl.BlockSpec((rows, group_size * HD), lambda h, ids: (0, h))
    kwblock = pl.BlockSpec((window, HD), lambda h, ids: (0, h))
    vwblock = pl.BlockSpec((window, HD), lambda h, ids: (0, h + kv_heads))
    kbblock = pl.BlockSpec((beacon_total, HD), lambda h, ids: (0, h))
    vbblock = pl.BlockSpec((beacon_total, HD), lambda h, ids: (0, h + kv_heads))
    wgblock = pl.BlockSpec((window, 2 * HD), lambda h, ids: (0, h))
    bgblock = pl.BlockSpec((beacon_total, 2 * HD), lambda h, ids: (0, h))
    return pl.pallas_call(
        kernel,
        grid_spec=pltpu.PrefetchScalarGridSpec(
            num_scalar_prefetch=1,
            grid=(kv_heads,),
            in_specs=[qblock, qblock, kwblock, vwblock, kbblock, vbblock],
            out_specs=[wgblock, bgblock, qblock, qblock],
        ),
        out_shape=[
            jax.ShapeDtypeStruct((window, kv_double), jnp.float32),
            jax.ShapeDtypeStruct((beacon_total, kv_double), jnp.bfloat16),
            jax.ShapeDtypeStruct((rows, q_width), jnp.bfloat16),
            jax.ShapeDtypeStruct((rows, q_width), jnp.bfloat16),
        ],
    )(ids, queries, out_grad, kv_window, kv_window, kv_beacons, kv_beacons)


def head_gather(block, axis, count):
    index = lax.axis_index(axis)
    from_left, from_right = [block], [block]
    for step in range(1, count):
        from_left.append(
            lax.ppermute(from_left[-1], axis, [(j, j + 1) for j in range(step - 1, count - 1)])
        )
        from_right.append(
            lax.ppermute(from_right[-1], axis, [(j + 1, j) for j in range(count - step)])
        )
    pieces = jnp.stack(from_left + from_right[1:])
    order = jnp.arange(count)
    pick = jnp.where(order <= index, index - order, count - 1 + order - index)
    return pieces[pick].reshape((count * block.shape[0],) + block.shape[1:])


def head_reduce(partials, axis, count):
    index = lax.axis_index(axis)
    rows = partials.shape[0] // count

    def block_of(target):
        return lax.dynamic_slice_in_dim(partials, jnp.clip(target, 0, count - 1) * rows, rows, 0)

    left = jnp.zeros((rows, partials.shape[1]), jnp.bfloat16)
    right = jnp.zeros((rows, partials.shape[1]), jnp.bfloat16)
    for step in range(1, count):
        send_left = (block_of(index + step - count) + left.astype(jnp.float32)).astype(jnp.bfloat16)
        send_right = (block_of(index - step + count) + right.astype(jnp.float32)).astype(jnp.bfloat16)
        left = lax.ppermute(send_left, axis, [(j, j - 1) for j in range(max(1, count - step), count)])
        right = lax.ppermute(send_right, axis, [(j, j + 1) for j in range(0, min(step, count - 1))])
    return block_of(index) + left.astype(jnp.float32) + right.astype(jnp.float32)


def local_part(queries, keys, values, out_grad, positions, ids, heads_axis, ctx_axis, offload):
    kv_width = keys.shape[1]
    per_shard = positions.shape[0]
    kv_rows = jnp.concatenate([keys, values], axis=1)
    kv_window = head_gather(kv_rows, "head", heads_axis)
    window = kv_window.shape[0]
    own_beacon_rows = kv_window[positions]
    kv_beacons = lax.all_to_all(
        jnp.broadcast_to(own_beacon_rows[None], (ctx_axis,) + own_beacon_rows.shape),
        "ctx", 0, 0, tiled=True,
    ).reshape(ctx_axis * per_shard, 2 * kv_width)
    window_grads, beacon_grads, attended_out, query_out = attend_all(
        ids, queries, out_grad, kv_window, kv_beacons, per_shard
    )
    beacon_parts = lax.all_to_all(
        beacon_grads.reshape(ctx_axis, per_shard, 2 * kv_width), "ctx", 0, 0, tiled=True
    )
    own_beacons = jnp.sum(beacon_parts.astype(jnp.float32), axis=0)
    window_grads = window_grads.at[positions].add(own_beacons)
    if offload:
        own_grads = lax.psum_scatter(
            window_grads.astype(jnp.bfloat16), "head", scatter_dimension=0, tiled=True
        )
    else:
        own_grads = head_reduce(window_grads, "head", heads_axis).astype(jnp.bfloat16)
    own_grads = own_grads.reshape(own_grads.shape[0], kv_width // HD, 2, HD)
    rows = own_grads.shape[0]
    return (
        attended_out, query_out,
        own_grads[:, :, 0].reshape(rows, kv_width), own_grads[:, :, 1].reshape(rows, kv_width),
    )


def local(queries, keys, values, out_grad, beacon_pos, *, heads_axis, ctx_axis, parts):
    head_id = lax.axis_index("head")
    shard_id = lax.axis_index("ctx")
    ids = jnp.stack([head_id, shard_id]).astype(jnp.int32)
    positions = beacon_pos[0]
    q_cols = queries.shape[1] // parts
    kv_cols = keys.shape[1] // parts
    results = []
    for part in range(parts):
        qs = slice(part * q_cols, (part + 1) * q_cols)
        ks = slice(part * kv_cols, (part + 1) * kv_cols)
        results.append(
            local_part(
                queries[:, qs], keys[:, ks], values[:, ks], out_grad[:, qs],
                positions, ids, heads_axis, ctx_axis, part + 1 < parts,
            )
        )
    return tuple(jnp.concatenate(outs, axis=1) for outs in zip(*results))


def solution(mesh):
    in_specs = (
        P(("ctx", "head"), None),
        P(("ctx", "head"), None),
        P(("ctx", "head"), None),
        P(("ctx", "head"), None),
        P("ctx", None),
    )
    out_specs = (
        P(("ctx", "head"), None),
        P(("ctx", "head"), None),
        P(("ctx", "head"), None),
        P(("ctx", "head"), None),
    )
    body = functools.partial(local, heads_axis=mesh.shape["head"], ctx_axis=mesh.shape["ctx"], parts=2)
    return jax.shard_map(body, mesh=mesh, in_specs=in_specs, out_specs=out_specs, check_vma=False)
```

```python
import functools
import jax
import jax.numpy as jnp
from jax import lax
from jax.experimental import pallas as pl
from jax.experimental.pallas import tpu as pltpu
from jax.sharding import PartitionSpec as P

HD = 128


NEG_FILL = -1e30


def attention_kernel(
    ids_ref, q_ref, g_ref, kw_ref, vw_ref, kb_ref, vb_ref, wgrad_ref, bgrad_ref,
    att_ref, dq_ref, *, rows, window, per_shard, group_size
):
    scaling = HD ** (-0.5)
    head_id = ids_ref[0]
    shard_id = ids_ref[1]
    k = jnp.concatenate([kw_ref[...], kb_ref[...]], axis=0)
    v = jnp.concatenate([vw_ref[...], vb_ref[...]], axis=0)
    key_count = k.shape[0]
    stacked = rows * group_size
    row = lax.rem(lax.broadcasted_iota(jnp.int32, (stacked, key_count), 0), rows) + head_id * rows
    col = lax.broadcasted_iota(jnp.int32, (stacked, key_count), 1)
    in_window = col < window
    visible = (in_window & (row >= col)) | (
        jnp.logical_not(in_window) & (col < window + shard_id * per_shard)
    )
    nt = (((1,), (1,)), ((), ()))
    tn = (((0,), (0,)), ((), ()))
    q = jnp.concatenate([q_ref[:, g * HD:(g + 1) * HD] for g in range(group_size)], axis=0)
    do = jnp.concatenate([g_ref[:, g * HD:(g + 1) * HD] for g in range(group_size)], axis=0)
    scores = lax.dot_general(q, k, nt, preferred_element_type=jnp.float32) * scaling
    scores = jnp.where(visible, scores, NEG_FILL)
    row_max = jnp.max(scores, axis=1, keepdims=True)
    weights = jnp.exp(scores - row_max)
    probs = weights / jnp.sum(weights, axis=1, keepdims=True)
    probs_low = probs.astype(jnp.bfloat16)
    attended = jnp.dot(probs_low, v, preferred_element_type=jnp.float32).astype(jnp.bfloat16)
    row_dot = jnp.sum(do.astype(jnp.float32) * attended.astype(jnp.float32), axis=1, keepdims=True)
    dprob = lax.dot_general(do, v, nt, preferred_element_type=jnp.float32)
    grad_scores = (probs * (dprob - row_dot)).astype(jnp.bfloat16)
    query_grad = (
        jnp.dot(grad_scores, k, preferred_element_type=jnp.float32) * scaling
    ).astype(jnp.bfloat16)
    for g in range(group_size):
        att_ref[:, g * HD:(g + 1) * HD] = attended[g * rows:(g + 1) * rows]
        dq_ref[:, g * HD:(g + 1) * HD] = query_grad[g * rows:(g + 1) * rows]
    key_grad = (lax.dot_general(q, grad_scores, tn, preferred_element_type=jnp.float32) * scaling).T
    value_grad = lax.dot_general(do, probs_low, tn, preferred_element_type=jnp.float32).T
    wgrad_ref[:, :HD] = key_grad[:window]
    wgrad_ref[:, HD:] = value_grad[:window]
    bgrad_ref[:, :HD] = key_grad[window:].astype(jnp.bfloat16)
    bgrad_ref[:, HD:] = value_grad[window:].astype(jnp.bfloat16)


def attend_all(ids, queries, out_grad, kv_window, kv_beacons, per_shard, part, parts):
    rows, q_width = queries.shape
    q_width = q_width // parts
    window, kv_double = kv_window.shape
    beacon_total = kv_beacons.shape[0]
    kv_heads = kv_double // 2 // HD
    group_size = q_width // HD // kv_heads
    kernel = functools.partial(
        attention_kernel, rows=rows, window=window, per_shard=per_shard, group_size=group_size
    )
    qinblock = pl.BlockSpec((rows, group_size * HD), lambda h, ids: (0, h + part * kv_heads))
    qblock = pl.BlockSpec((rows, group_size * HD), lambda h, ids: (0, h))
    kwblock = pl.BlockSpec((window, HD), lambda h, ids: (0, h))
    vwblock = pl.BlockSpec((window, HD), lambda h, ids: (0, h + kv_heads))
    kbblock = pl.BlockSpec((beacon_total, HD), lambda h, ids: (0, h))
    vbblock = pl.BlockSpec((beacon_total, HD), lambda h, ids: (0, h + kv_heads))
    wgblock = pl.BlockSpec((window, 2 * HD), lambda h, ids: (0, h))
    bgblock = pl.BlockSpec((beacon_total, 2 * HD), lambda h, ids: (0, h))
    return pl.pallas_call(
        kernel,
        grid_spec=pltpu.PrefetchScalarGridSpec(
            num_scalar_prefetch=1,
            grid=(kv_heads,),
            in_specs=[qinblock, qinblock, kwblock, vwblock, kbblock, vbblock],
            out_specs=[wgblock, bgblock, qblock, qblock],
        ),
        out_shape=[
            jax.ShapeDtypeStruct((window, kv_double), jnp.float32),
            jax.ShapeDtypeStruct((beacon_total, kv_double), jnp.bfloat16),
            jax.ShapeDtypeStruct((rows, q_width), jnp.bfloat16),
            jax.ShapeDtypeStruct((rows, q_width), jnp.bfloat16),
        ],
    )(ids, queries, out_grad, kv_window, kv_window, kv_beacons, kv_beacons)


def head_gather(block, axis, count):
    index = lax.axis_index(axis)
    from_left, from_right = [block], [block]
    for step in range(1, count):
        from_left.append(
            lax.ppermute(from_left[-1], axis, [(j, j + 1) for j in range(step - 1, count - 1)])
        )
        from_right.append(
            lax.ppermute(from_right[-1], axis, [(j + 1, j) for j in range(count - step)])
        )
    pieces = jnp.stack(from_left + from_right[1:])
    order = jnp.arange(count)
    pick = jnp.where(order <= index, index - order, count - 1 + order - index)
    return pieces[pick].reshape((count * block.shape[0],) + block.shape[1:])


def head_reduce(partials, axis, count):
    index = lax.axis_index(axis)
    rows = partials.shape[0] // count

    def block_of(target):
        return lax.dynamic_slice_in_dim(partials, jnp.clip(target, 0, count - 1) * rows, rows, 0)

    left = jnp.zeros((rows, partials.shape[1]), jnp.bfloat16)
    right = jnp.zeros((rows, partials.shape[1]), jnp.bfloat16)
    for step in range(1, count):
        send_left = (block_of(index + step - count) + left.astype(jnp.float32)).astype(jnp.bfloat16)
        send_right = (block_of(index - step + count) + right.astype(jnp.float32)).astype(jnp.bfloat16)
        left = lax.ppermute(send_left, axis, [(j, j - 1) for j in range(max(1, count - step), count)])
        right = lax.ppermute(send_right, axis, [(j, j + 1) for j in range(0, min(step, count - 1))])
    return block_of(index) + left.astype(jnp.float32) + right.astype(jnp.float32)


def local_part(queries, keys, values, out_grad, positions, ids, heads_axis, ctx_axis, part, parts):
    kv_width = keys.shape[1]
    per_shard = positions.shape[0]
    kv_rows = jnp.concatenate([keys, values], axis=1)
    kv_window = head_gather(kv_rows, "head", heads_axis)
    window = kv_window.shape[0]
    own_beacon_rows = kv_window[positions]
    kv_beacons = lax.all_to_all(
        jnp.broadcast_to(own_beacon_rows[None], (ctx_axis,) + own_beacon_rows.shape),
        "ctx", 0, 0, tiled=True,
    ).reshape(ctx_axis * per_shard, 2 * kv_width)
    window_grads, beacon_grads, attended_out, query_out = attend_all(
        ids, queries, out_grad, kv_window, kv_beacons, per_shard, part, parts
    )
    beacon_parts = lax.all_to_all(
        beacon_grads.reshape(ctx_axis, per_shard, 2 * kv_width), "ctx", 0, 0, tiled=True
    )
    own_beacons = jnp.sum(beacon_parts.astype(jnp.float32), axis=0)
    window_grads = window_grads.at[positions].add(own_beacons)
    own_grads = head_reduce(window_grads, "head", heads_axis).astype(jnp.bfloat16)
    own_grads = own_grads.reshape(own_grads.shape[0], kv_width // HD, 2, HD)
    rows = own_grads.shape[0]
    return (
        attended_out, query_out,
        own_grads[:, :, 0].reshape(rows, kv_width), own_grads[:, :, 1].reshape(rows, kv_width),
    )


def local(queries, keys, values, out_grad, beacon_pos, *, heads_axis, ctx_axis, parts):
    head_id = lax.axis_index("head")
    shard_id = lax.axis_index("ctx")
    ids = jnp.stack([head_id, shard_id]).astype(jnp.int32)
    positions = beacon_pos[0]
    q_cols = queries.shape[1] // parts
    kv_cols = keys.shape[1] // parts
    results = []
    for part in range(parts):
        qs = slice(part * q_cols, (part + 1) * q_cols)
        ks = slice(part * kv_cols, (part + 1) * kv_cols)
        results.append(
            local_part(
                queries, keys[:, ks], values[:, ks], out_grad,
                positions, ids, heads_axis, ctx_axis, part, parts,
            )
        )
    return tuple(jnp.concatenate(outs, axis=1) for outs in zip(*results))


def solution(mesh):
    in_specs = (
        P(("ctx", "head"), None),
        P(("ctx", "head"), None),
        P(("ctx", "head"), None),
        P(("ctx", "head"), None),
        P("ctx", None),
    )
    out_specs = (
        P(("ctx", "head"), None),
        P(("ctx", "head"), None),
        P(("ctx", "head"), None),
        P(("ctx", "head"), None),
    )
    body = functools.partial(local, heads_axis=mesh.shape["head"], ctx_axis=mesh.shape["ctx"], parts=2)
    return jax.shard_map(body, mesh=mesh, in_specs=in_specs, out_specs=out_specs, check_vma=False)
```

```python
import functools
import jax
import jax.numpy as jnp
from jax import lax
from jax.experimental import pallas as pl
from jax.experimental.pallas import tpu as pltpu
from jax.sharding import PartitionSpec as P

HD = 128


NEG_FILL = -1e30


def attention_kernel(
    ids_ref, q_ref, g_ref, kw_ref, vw_ref, kb_ref, vb_ref, wgrad_ref, bgrad_ref,
    att_ref, dq_ref, *, rows, window, per_shard, group_size
):
    scaling = HD ** (-0.5)
    head_id = ids_ref[0]
    shard_id = ids_ref[1]
    k = jnp.concatenate([kw_ref[...], kb_ref[...]], axis=0)
    v = jnp.concatenate([vw_ref[...], vb_ref[...]], axis=0)
    key_count = k.shape[0]
    stacked = rows * group_size
    row = lax.rem(lax.broadcasted_iota(jnp.int32, (stacked, key_count), 0), rows) + head_id * rows
    col = lax.broadcasted_iota(jnp.int32, (stacked, key_count), 1)
    in_window = col < window
    visible = (in_window & (row >= col)) | (
        jnp.logical_not(in_window) & (col < window + shard_id * per_shard)
    )
    nt = (((1,), (1,)), ((), ()))
    tn = (((0,), (0,)), ((), ()))
    q = jnp.concatenate([q_ref[:, g * HD:(g + 1) * HD] for g in range(group_size)], axis=0)
    do = jnp.concatenate([g_ref[:, g * HD:(g + 1) * HD] for g in range(group_size)], axis=0)
    scores = lax.dot_general(q, k, nt, preferred_element_type=jnp.float32) * scaling
    scores = jnp.where(visible, scores, NEG_FILL)
    row_max = jnp.max(scores, axis=1, keepdims=True)
    weights = jnp.exp(scores - row_max)
    probs = weights / jnp.sum(weights, axis=1, keepdims=True)
    probs_low = probs.astype(jnp.bfloat16)
    attended = jnp.dot(probs_low, v, preferred_element_type=jnp.float32).astype(jnp.bfloat16)
    row_dot = jnp.sum(do.astype(jnp.float32) * attended.astype(jnp.float32), axis=1, keepdims=True)
    dprob = lax.dot_general(do, v, nt, preferred_element_type=jnp.float32)
    grad_scores = (probs * (dprob - row_dot)).astype(jnp.bfloat16)
    query_grad = (
        jnp.dot(grad_scores, k, preferred_element_type=jnp.float32) * scaling
    ).astype(jnp.bfloat16)
    for g in range(group_size):
        att_ref[:, g * HD:(g + 1) * HD] = attended[g * rows:(g + 1) * rows]
        dq_ref[:, g * HD:(g + 1) * HD] = query_grad[g * rows:(g + 1) * rows]
    key_grad = (lax.dot_general(q, grad_scores, tn, preferred_element_type=jnp.float32) * scaling).T
    value_grad = lax.dot_general(do, probs_low, tn, preferred_element_type=jnp.float32).T
    wgrad_ref[:, :HD] = key_grad[:window]
    wgrad_ref[:, HD:] = value_grad[:window]
    bgrad_ref[:, :HD] = key_grad[window:].astype(jnp.bfloat16)
    bgrad_ref[:, HD:] = value_grad[window:].astype(jnp.bfloat16)


def attend_all(ids, queries, out_grad, kv_window, kv_beacons, per_shard, part, parts):
    rows, q_width = queries.shape
    q_width = q_width // parts
    window, kv_double = kv_window.shape
    beacon_total = kv_beacons.shape[0]
    kv_heads = kv_double // 2 // HD
    group_size = q_width // HD // kv_heads
    kernel = functools.partial(
        attention_kernel, rows=rows, window=window, per_shard=per_shard, group_size=group_size
    )
    qinblock = pl.BlockSpec((rows, group_size * HD), lambda h, ids: (0, h + part * kv_heads))
    qblock = pl.BlockSpec((rows, group_size * HD), lambda h, ids: (0, h))
    kwblock = pl.BlockSpec((window, HD), lambda h, ids: (0, h))
    vwblock = pl.BlockSpec((window, HD), lambda h, ids: (0, h + kv_heads))
    kbblock = pl.BlockSpec((beacon_total, HD), lambda h, ids: (0, h))
    vbblock = pl.BlockSpec((beacon_total, HD), lambda h, ids: (0, h + kv_heads))
    wgblock = pl.BlockSpec((window, 2 * HD), lambda h, ids: (0, h))
    bgblock = pl.BlockSpec((beacon_total, 2 * HD), lambda h, ids: (0, h))
    return pl.pallas_call(
        kernel,
        grid_spec=pltpu.PrefetchScalarGridSpec(
            num_scalar_prefetch=1,
            grid=(kv_heads,),
            in_specs=[qinblock, qinblock, kwblock, vwblock, kbblock, vbblock],
            out_specs=[wgblock, bgblock, qblock, qblock],
        ),
        out_shape=[
            jax.ShapeDtypeStruct((window, kv_double), jnp.float32),
            jax.ShapeDtypeStruct((beacon_total, kv_double), jnp.bfloat16),
            jax.ShapeDtypeStruct((rows, q_width), jnp.bfloat16),
            jax.ShapeDtypeStruct((rows, q_width), jnp.bfloat16),
        ],
    )(ids, queries, out_grad, kv_window, kv_window, kv_beacons, kv_beacons)


def head_gather(block, axis, count):
    index = lax.axis_index(axis)
    from_left, from_right = [block], [block]
    for step in range(1, count):
        from_left.append(
            lax.ppermute(from_left[-1], axis, [(j, j + 1) for j in range(step - 1, count - 1)])
        )
        from_right.append(
            lax.ppermute(from_right[-1], axis, [(j + 1, j) for j in range(count - step)])
        )
    pieces = jnp.stack(from_left + from_right[1:])
    window = []
    for order in range(count):
        pick = jnp.where(order <= index, index - order, count - 1 + order - index)
        window.append(lax.dynamic_index_in_dim(pieces, pick, 0, keepdims=False))
    return jnp.concatenate(window, axis=0)


def head_reduce(partials, axis, count):
    index = lax.axis_index(axis)
    rows = partials.shape[0] // count

    def block_of(target):
        return lax.dynamic_slice_in_dim(partials, jnp.clip(target, 0, count - 1) * rows, rows, 0)

    left = jnp.zeros((rows, partials.shape[1]), jnp.bfloat16)
    right = jnp.zeros((rows, partials.shape[1]), jnp.bfloat16)
    for step in range(1, count):
        send_left = (block_of(index + step - count) + left.astype(jnp.float32)).astype(jnp.bfloat16)
        send_right = (block_of(index - step + count) + right.astype(jnp.float32)).astype(jnp.bfloat16)
        left = lax.ppermute(send_left, axis, [(j, j - 1) for j in range(max(1, count - step), count)])
        right = lax.ppermute(send_right, axis, [(j, j + 1) for j in range(0, min(step, count - 1))])
    return block_of(index) + left.astype(jnp.float32) + right.astype(jnp.float32)


def local_part(queries, keys, values, out_grad, positions, ids, heads_axis, ctx_axis, part, parts):
    kv_width = keys.shape[1]
    per_shard = positions.shape[0]
    kv_rows = jnp.concatenate([keys, values], axis=1)
    kv_window = head_gather(kv_rows, "head", heads_axis)
    window = kv_window.shape[0]
    own_beacon_rows = kv_window[positions]
    kv_beacons = lax.all_to_all(
        jnp.broadcast_to(own_beacon_rows[None], (ctx_axis,) + own_beacon_rows.shape),
        "ctx", 0, 0, tiled=True,
    ).reshape(ctx_axis * per_shard, 2 * kv_width)
    window_grads, beacon_grads, attended_out, query_out = attend_all(
        ids, queries, out_grad, kv_window, kv_beacons, per_shard, part, parts
    )
    beacon_parts = lax.all_to_all(
        beacon_grads.reshape(ctx_axis, per_shard, 2 * kv_width), "ctx", 0, 0, tiled=True
    )
    own_beacons = jnp.sum(beacon_parts.astype(jnp.float32), axis=0)
    window_grads = window_grads.at[positions].add(own_beacons)
    own_grads = head_reduce(window_grads, "head", heads_axis).astype(jnp.bfloat16)
    own_grads = own_grads.reshape(own_grads.shape[0], kv_width // HD, 2, HD)
    rows = own_grads.shape[0]
    return (
        attended_out, query_out,
        own_grads[:, :, 0].reshape(rows, kv_width), own_grads[:, :, 1].reshape(rows, kv_width),
    )


def local(queries, keys, values, out_grad, beacon_pos, *, heads_axis, ctx_axis, parts):
    head_id = lax.axis_index("head")
    shard_id = lax.axis_index("ctx")
    ids = jnp.stack([head_id, shard_id]).astype(jnp.int32)
    positions = beacon_pos[0]
    q_cols = queries.shape[1] // parts
    kv_cols = keys.shape[1] // parts
    results = []
    for part in range(parts):
        qs = slice(part * q_cols, (part + 1) * q_cols)
        ks = slice(part * kv_cols, (part + 1) * kv_cols)
        results.append(
            local_part(
                queries, keys[:, ks], values[:, ks], out_grad,
                positions, ids, heads_axis, ctx_axis, part, parts,
            )
        )
    return tuple(jnp.concatenate(outs, axis=1) for outs in zip(*results))


def solution(mesh):
    in_specs = (
        P(("ctx", "head"), None),
        P(("ctx", "head"), None),
        P(("ctx", "head"), None),
        P(("ctx", "head"), None),
        P("ctx", None),
    )
    out_specs = (
        P(("ctx", "head"), None),
        P(("ctx", "head"), None),
        P(("ctx", "head"), None),
        P(("ctx", "head"), None),
    )
    body = functools.partial(local, heads_axis=mesh.shape["head"], ctx_axis=mesh.shape["ctx"], parts=2)
    return jax.shard_map(body, mesh=mesh, in_specs=in_specs, out_specs=out_specs, check_vma=False)
```

```python
import functools
import jax
import jax.numpy as jnp
from jax import lax
from jax.experimental import pallas as pl
from jax.experimental.pallas import tpu as pltpu
from jax.sharding import PartitionSpec as P

HD = 128


NEG_FILL = -1e30


def attention_kernel(
    ids_ref, q_ref, g_ref, kw_ref, vw_ref, kb_ref, vb_ref, *refs, rows, window, per_shard, group_size
):
    wgrad_ref, bgrad_ref, att_ref, dq_ref = refs[-4:]
    scaling = HD ** (-0.5)
    head_id = ids_ref[0]
    shard_id = ids_ref[1]
    k = jnp.concatenate([kw_ref[...], kb_ref[...]], axis=0)
    v = jnp.concatenate([vw_ref[...], vb_ref[...]], axis=0)
    key_count = k.shape[0]
    stacked = rows * group_size
    row = lax.rem(lax.broadcasted_iota(jnp.int32, (stacked, key_count), 0), rows) + head_id * rows
    col = lax.broadcasted_iota(jnp.int32, (stacked, key_count), 1)
    in_window = col < window
    visible = (in_window & (row >= col)) | (
        jnp.logical_not(in_window) & (col < window + shard_id * per_shard)
    )
    nt = (((1,), (1,)), ((), ()))
    tn = (((0,), (0,)), ((), ()))
    q = jnp.concatenate([q_ref[:, g * HD:(g + 1) * HD] for g in range(group_size)], axis=0)
    do = jnp.concatenate([g_ref[:, g * HD:(g + 1) * HD] for g in range(group_size)], axis=0)
    scores = lax.dot_general(q, k, nt, preferred_element_type=jnp.float32) * scaling
    scores = jnp.where(visible, scores, NEG_FILL)
    row_max = jnp.max(scores, axis=1, keepdims=True)
    weights = jnp.exp(scores - row_max)
    probs = weights / jnp.sum(weights, axis=1, keepdims=True)
    probs_low = probs.astype(jnp.bfloat16)
    attended = jnp.dot(probs_low, v, preferred_element_type=jnp.float32).astype(jnp.bfloat16)
    row_dot = jnp.sum(do.astype(jnp.float32) * attended.astype(jnp.float32), axis=1, keepdims=True)
    dprob = lax.dot_general(do, v, nt, preferred_element_type=jnp.float32)
    grad_scores = (probs * (dprob - row_dot)).astype(jnp.bfloat16)
    query_grad = (
        jnp.dot(grad_scores, k, preferred_element_type=jnp.float32) * scaling
    ).astype(jnp.bfloat16)
    for g in range(group_size):
        att_ref[:, g * HD:(g + 1) * HD] = attended[g * rows:(g + 1) * rows]
        dq_ref[:, g * HD:(g + 1) * HD] = query_grad[g * rows:(g + 1) * rows]
    key_grad = (lax.dot_general(q, grad_scores, tn, preferred_element_type=jnp.float32) * scaling).T
    value_grad = lax.dot_general(do, probs_low, tn, preferred_element_type=jnp.float32).T
    wgrad_ref[:, :HD] = key_grad[:window]
    wgrad_ref[:, HD:] = value_grad[:window]
    bgrad_ref[:, :HD] = key_grad[window:].astype(jnp.bfloat16)
    bgrad_ref[:, HD:] = value_grad[window:].astype(jnp.bfloat16)


def attend_all(ids, queries, out_grad, kv_window, kv_beacons, per_shard, part, parts, earlier):
    rows, q_width = queries.shape
    q_width = q_width // parts
    window, kv_double = kv_window.shape
    beacon_total = kv_beacons.shape[0]
    kv_heads = kv_double // 2 // HD
    group_size = q_width // HD // kv_heads
    kernel = functools.partial(
        attention_kernel, rows=rows, window=window, per_shard=per_shard, group_size=group_size
    )
    qinblock = pl.BlockSpec((rows, group_size * HD), lambda h, ids: (0, h + part * kv_heads))
    qblock = pl.BlockSpec((rows, group_size * HD), lambda h, ids: (0, h + part * kv_heads))
    kwblock = pl.BlockSpec((window, HD), lambda h, ids: (0, h))
    vwblock = pl.BlockSpec((window, HD), lambda h, ids: (0, h + kv_heads))
    kbblock = pl.BlockSpec((beacon_total, HD), lambda h, ids: (0, h))
    vbblock = pl.BlockSpec((beacon_total, HD), lambda h, ids: (0, h + kv_heads))
    wgblock = pl.BlockSpec((window, 2 * HD), lambda h, ids: (0, h))
    bgblock = pl.BlockSpec((beacon_total, 2 * HD), lambda h, ids: (0, h))
    return pl.pallas_call(
        kernel,
        grid_spec=pltpu.PrefetchScalarGridSpec(
            num_scalar_prefetch=1,
            grid=(kv_heads,),
            in_specs=[qinblock, qinblock, kwblock, vwblock, kbblock, vbblock]
            + [pl.BlockSpec(memory_space=pl.ANY) for _ in earlier],
            out_specs=[wgblock, bgblock, qblock, qblock],
        ),
        out_shape=[
            jax.ShapeDtypeStruct((window, kv_double), jnp.float32),
            jax.ShapeDtypeStruct((beacon_total, kv_double), jnp.bfloat16),
            jax.ShapeDtypeStruct((rows, q_width * parts), jnp.bfloat16),
            jax.ShapeDtypeStruct((rows, q_width * parts), jnp.bfloat16),
        ],
        input_output_aliases={7 + i: 2 + i for i in range(len(earlier))},
    )(ids, queries, out_grad, kv_window, kv_window, kv_beacons, kv_beacons, *earlier)


def head_gather(block, axis, count):
    index = lax.axis_index(axis)
    from_left, from_right = [block], [block]
    for step in range(1, count):
        from_left.append(
            lax.ppermute(from_left[-1], axis, [(j, j + 1) for j in range(step - 1, count - 1)])
        )
        from_right.append(
            lax.ppermute(from_right[-1], axis, [(j + 1, j) for j in range(count - step)])
        )
    pieces = jnp.stack(from_left + from_right[1:])
    window = []
    for order in range(count):
        pick = jnp.where(order <= index, index - order, count - 1 + order - index)
        window.append(lax.dynamic_index_in_dim(pieces, pick, 0, keepdims=False))
    return jnp.concatenate(window, axis=0)


def head_reduce(partials, axis, count):
    index = lax.axis_index(axis)
    rows = partials.shape[0] // count

    def block_of(target):
        return lax.dynamic_slice_in_dim(partials, jnp.clip(target, 0, count - 1) * rows, rows, 0)

    left = jnp.zeros((rows, partials.shape[1]), jnp.bfloat16)
    right = jnp.zeros((rows, partials.shape[1]), jnp.bfloat16)
    for step in range(1, count):
        send_left = (block_of(index + step - count) + left.astype(jnp.float32)).astype(jnp.bfloat16)
        send_right = (block_of(index - step + count) + right.astype(jnp.float32)).astype(jnp.bfloat16)
        left = lax.ppermute(send_left, axis, [(j, j - 1) for j in range(max(1, count - step), count)])
        right = lax.ppermute(send_right, axis, [(j, j + 1) for j in range(0, min(step, count - 1))])
    return block_of(index) + left.astype(jnp.float32) + right.astype(jnp.float32)


def local_part(queries, keys, values, out_grad, positions, ids, heads_axis, ctx_axis, part, parts, earlier):
    kv_width = keys.shape[1]
    per_shard = positions.shape[0]
    kv_rows = jnp.concatenate([keys, values], axis=1)
    kv_window = head_gather(kv_rows, "head", heads_axis)
    window = kv_window.shape[0]
    own_beacon_rows = kv_window[positions]
    kv_beacons = lax.all_to_all(
        jnp.broadcast_to(own_beacon_rows[None], (ctx_axis,) + own_beacon_rows.shape),
        "ctx", 0, 0, tiled=True,
    ).reshape(ctx_axis * per_shard, 2 * kv_width)
    window_grads, beacon_grads, attended_out, query_out = attend_all(
        ids, queries, out_grad, kv_window, kv_beacons, per_shard, part, parts, earlier
    )
    beacon_parts = lax.all_to_all(
        beacon_grads.reshape(ctx_axis, per_shard, 2 * kv_width), "ctx", 0, 0, tiled=True
    )
    own_beacons = jnp.sum(beacon_parts.astype(jnp.float32), axis=0)
    window_grads = window_grads.at[positions].add(own_beacons)
    own_grads = head_reduce(window_grads, "head", heads_axis).astype(jnp.bfloat16)
    own_grads = own_grads.reshape(own_grads.shape[0], kv_width // HD, 2, HD)
    rows = own_grads.shape[0]
    return (
        attended_out, query_out,
        own_grads[:, :, 0].reshape(rows, kv_width), own_grads[:, :, 1].reshape(rows, kv_width),
    )


def local(queries, keys, values, out_grad, beacon_pos, *, heads_axis, ctx_axis, parts):
    head_id = lax.axis_index("head")
    shard_id = lax.axis_index("ctx")
    ids = jnp.stack([head_id, shard_id]).astype(jnp.int32)
    positions = beacon_pos[0]
    q_cols = queries.shape[1] // parts
    kv_cols = keys.shape[1] // parts
    results = []
    for part in range(parts):
        qs = slice(part * q_cols, (part + 1) * q_cols)
        ks = slice(part * kv_cols, (part + 1) * kv_cols)
        results.append(
            local_part(
                queries, keys[:, ks], values[:, ks], out_grad,
                positions, ids, heads_axis, ctx_axis, part, parts,
                results[-1][:2] if results else (),
            )
        )
    key_grad, value_grad = (jnp.concatenate(outs, axis=1) for outs in list(zip(*results))[2:])
    return results[-1][0], results[-1][1], key_grad, value_grad


def solution(mesh):
    in_specs = (
        P(("ctx", "head"), None),
        P(("ctx", "head"), None),
        P(("ctx", "head"), None),
        P(("ctx", "head"), None),
        P("ctx", None),
    )
    out_specs = (
        P(("ctx", "head"), None),
        P(("ctx", "head"), None),
        P(("ctx", "head"), None),
        P(("ctx", "head"), None),
    )
    body = functools.partial(local, heads_axis=mesh.shape["head"], ctx_axis=mesh.shape["ctx"], parts=2)
    return jax.shard_map(body, mesh=mesh, in_specs=in_specs, out_specs=out_specs, check_vma=False)
```

```python
import functools
import jax
import jax.numpy as jnp
from jax import lax
from jax.experimental import pallas as pl
from jax.experimental.pallas import tpu as pltpu
from jax.sharding import PartitionSpec as P

HD = 128


NEG_FILL = -1e30


def attention_kernel(
    ids_ref, q_ref, g_ref, kw_ref, vw_ref, kb_ref, vb_ref, *refs, rows, window, per_shard, group_size
):
    wgrad_ref, bgrad_ref, att_ref, dq_ref = refs[-4:]
    scaling = HD ** (-0.5)
    head_id = ids_ref[0]
    shard_id = ids_ref[1]
    k = jnp.concatenate([kw_ref[...], kb_ref[...]], axis=0)
    v = jnp.concatenate([vw_ref[...], vb_ref[...]], axis=0)
    key_count = k.shape[0]
    row = lax.broadcasted_iota(jnp.int32, (rows, key_count), 0) + head_id * rows
    col = lax.broadcasted_iota(jnp.int32, (rows, key_count), 1)
    in_window = col < window
    visible = (in_window & (row >= col)) | (
        jnp.logical_not(in_window) & (col < window + shard_id * per_shard)
    )
    hidden = jnp.where(visible, 0.0, NEG_FILL).astype(jnp.float32)
    hidden = jnp.concatenate([hidden] * group_size, axis=0)
    nt = (((1,), (1,)), ((), ()))
    tn = (((0,), (0,)), ((), ()))
    q = jnp.concatenate([q_ref[:, g * HD:(g + 1) * HD] for g in range(group_size)], axis=0)
    do = jnp.concatenate([g_ref[:, g * HD:(g + 1) * HD] for g in range(group_size)], axis=0)
    scores = lax.dot_general(q, k, nt, preferred_element_type=jnp.float32) * scaling
    scores = scores + hidden
    row_max = jnp.max(scores, axis=1, keepdims=True)
    weights = jnp.exp(scores - row_max)
    probs = weights / jnp.sum(weights, axis=1, keepdims=True)
    probs_low = probs.astype(jnp.bfloat16)
    attended = jnp.dot(probs_low, v, preferred_element_type=jnp.float32).astype(jnp.bfloat16)
    row_dot = jnp.sum(do.astype(jnp.float32) * attended.astype(jnp.float32), axis=1, keepdims=True)
    dprob = lax.dot_general(do, v, nt, preferred_element_type=jnp.float32)
    grad_scores = (probs * (dprob - row_dot)).astype(jnp.bfloat16)
    query_grad = (
        jnp.dot(grad_scores, k, preferred_element_type=jnp.float32) * scaling
    ).astype(jnp.bfloat16)
    for g in range(group_size):
        att_ref[:, g * HD:(g + 1) * HD] = attended[g * rows:(g + 1) * rows]
        dq_ref[:, g * HD:(g + 1) * HD] = query_grad[g * rows:(g + 1) * rows]
    key_grad = (lax.dot_general(q, grad_scores, tn, preferred_element_type=jnp.float32) * scaling).T
    value_grad = lax.dot_general(do, probs_low, tn, preferred_element_type=jnp.float32).T
    wgrad_ref[:, :HD] = key_grad[:window]
    wgrad_ref[:, HD:] = value_grad[:window]
    bgrad_ref[:, :HD] = key_grad[window:].astype(jnp.bfloat16)
    bgrad_ref[:, HD:] = value_grad[window:].astype(jnp.bfloat16)


def attend_all(ids, queries, out_grad, kv_window, kv_beacons, per_shard, part, parts, earlier):
    rows, q_width = queries.shape
    q_width = q_width // parts
    window, kv_double = kv_window.shape
    beacon_total = kv_beacons.shape[0]
    kv_heads = kv_double // 2 // HD
    group_size = q_width // HD // kv_heads
    kernel = functools.partial(
        attention_kernel, rows=rows, window=window, per_shard=per_shard, group_size=group_size
    )
    qinblock = pl.BlockSpec((rows, group_size * HD), lambda h, ids: (0, h + part * kv_heads))
    qblock = pl.BlockSpec((rows, group_size * HD), lambda h, ids: (0, h + part * kv_heads))
    kwblock = pl.BlockSpec((window, HD), lambda h, ids: (0, h))
    vwblock = pl.BlockSpec((window, HD), lambda h, ids: (0, h + kv_heads))
    kbblock = pl.BlockSpec((beacon_total, HD), lambda h, ids: (0, h))
    vbblock = pl.BlockSpec((beacon_total, HD), lambda h, ids: (0, h + kv_heads))
    wgblock = pl.BlockSpec((window, 2 * HD), lambda h, ids: (0, h))
    bgblock = pl.BlockSpec((beacon_total, 2 * HD), lambda h, ids: (0, h))
    return pl.pallas_call(
        kernel,
        grid_spec=pltpu.PrefetchScalarGridSpec(
            num_scalar_prefetch=1,
            grid=(kv_heads,),
            in_specs=[qinblock, qinblock, kwblock, vwblock, kbblock, vbblock]
            + [pl.BlockSpec(memory_space=pl.ANY) for _ in earlier],
            out_specs=[wgblock, bgblock, qblock, qblock],
        ),
        out_shape=[
            jax.ShapeDtypeStruct((window, kv_double), jnp.float32),
            jax.ShapeDtypeStruct((beacon_total, kv_double), jnp.bfloat16),
            jax.ShapeDtypeStruct((rows, q_width * parts), jnp.bfloat16),
            jax.ShapeDtypeStruct((rows, q_width * parts), jnp.bfloat16),
        ],
        input_output_aliases={7 + i: 2 + i for i in range(len(earlier))},
    )(ids, queries, out_grad, kv_window, kv_window, kv_beacons, kv_beacons, *earlier)


def head_gather(block, axis, count):
    index = lax.axis_index(axis)
    from_left, from_right = [block], [block]
    for step in range(1, count):
        from_left.append(
            lax.ppermute(from_left[-1], axis, [(j, j + 1) for j in range(step - 1, count - 1)])
        )
        from_right.append(
            lax.ppermute(from_right[-1], axis, [(j + 1, j) for j in range(count - step)])
        )
    pieces = jnp.stack(from_left + from_right[1:])
    window = []
    for order in range(count):
        pick = jnp.where(order <= index, index - order, count - 1 + order - index)
        window.append(lax.dynamic_index_in_dim(pieces, pick, 0, keepdims=False))
    return jnp.concatenate(window, axis=0)


def head_reduce(partials, axis, count):
    index = lax.axis_index(axis)
    rows = partials.shape[0] // count

    def block_of(target):
        return lax.dynamic_slice_in_dim(partials, jnp.clip(target, 0, count - 1) * rows, rows, 0)

    left = jnp.zeros((rows, partials.shape[1]), jnp.bfloat16)
    right = jnp.zeros((rows, partials.shape[1]), jnp.bfloat16)
    for step in range(1, count):
        send_left = (block_of(index + step - count) + left.astype(jnp.float32)).astype(jnp.bfloat16)
        send_right = (block_of(index - step + count) + right.astype(jnp.float32)).astype(jnp.bfloat16)
        left = lax.ppermute(send_left, axis, [(j, j - 1) for j in range(max(1, count - step), count)])
        right = lax.ppermute(send_right, axis, [(j, j + 1) for j in range(0, min(step, count - 1))])
    return block_of(index) + left.astype(jnp.float32) + right.astype(jnp.float32)


def local_part(queries, keys, values, out_grad, positions, ids, heads_axis, ctx_axis, part, parts, earlier):
    kv_width = keys.shape[1]
    per_shard = positions.shape[0]
    kv_rows = jnp.concatenate([keys, values], axis=1)
    kv_window = head_gather(kv_rows, "head", heads_axis)
    window = kv_window.shape[0]
    own_beacon_rows = kv_window[positions]
    kv_beacons = lax.all_to_all(
        jnp.broadcast_to(own_beacon_rows[None], (ctx_axis,) + own_beacon_rows.shape),
        "ctx", 0, 0, tiled=True,
    ).reshape(ctx_axis * per_shard, 2 * kv_width)
    window_grads, beacon_grads, attended_out, query_out = attend_all(
        ids, queries, out_grad, kv_window, kv_beacons, per_shard, part, parts, earlier
    )
    beacon_parts = lax.all_to_all(
        beacon_grads.reshape(ctx_axis, per_shard, 2 * kv_width), "ctx", 0, 0, tiled=True
    )
    own_beacons = jnp.sum(beacon_parts.astype(jnp.float32), axis=0)
    window_grads = window_grads.at[positions].add(own_beacons)
    own_grads = head_reduce(window_grads, "head", heads_axis).astype(jnp.bfloat16)
    own_grads = own_grads.reshape(own_grads.shape[0], kv_width // HD, 2, HD)
    rows = own_grads.shape[0]
    return (
        attended_out, query_out,
        own_grads[:, :, 0].reshape(rows, kv_width), own_grads[:, :, 1].reshape(rows, kv_width),
    )


def local(queries, keys, values, out_grad, beacon_pos, *, heads_axis, ctx_axis, parts):
    head_id = lax.axis_index("head")
    shard_id = lax.axis_index("ctx")
    ids = jnp.stack([head_id, shard_id]).astype(jnp.int32)
    positions = beacon_pos[0]
    q_cols = queries.shape[1] // parts
    kv_cols = keys.shape[1] // parts
    results = []
    for part in range(parts):
        qs = slice(part * q_cols, (part + 1) * q_cols)
        ks = slice(part * kv_cols, (part + 1) * kv_cols)
        results.append(
            local_part(
                queries, keys[:, ks], values[:, ks], out_grad,
                positions, ids, heads_axis, ctx_axis, part, parts,
                results[-1][:2] if results else (),
            )
        )
    key_grad, value_grad = (jnp.concatenate(outs, axis=1) for outs in list(zip(*results))[2:])
    return results[-1][0], results[-1][1], key_grad, value_grad


def solution(mesh):
    in_specs = (
        P(("ctx", "head"), None),
        P(("ctx", "head"), None),
        P(("ctx", "head"), None),
        P(("ctx", "head"), None),
        P("ctx", None),
    )
    out_specs = (
        P(("ctx", "head"), None),
        P(("ctx", "head"), None),
        P(("ctx", "head"), None),
        P(("ctx", "head"), None),
    )
    body = functools.partial(local, heads_axis=mesh.shape["head"], ctx_axis=mesh.shape["ctx"], parts=2)
    return jax.shard_map(body, mesh=mesh, in_specs=in_specs, out_specs=out_specs, check_vma=False)
```

```python
import functools
import jax
import jax.numpy as jnp
from jax import lax
from jax.experimental import pallas as pl
from jax.experimental.pallas import tpu as pltpu
from jax.sharding import PartitionSpec as P

HD = 128


NEG_FILL = -1e30


def attention_kernel(
    ids_ref, q_ref, g_ref, kw_ref, vw_ref, kb_ref, vb_ref, *refs, rows, window, per_shard, group_size
):
    wgrad_ref, bgrad_ref, att_ref, dq_ref = refs[-4:]
    scaling = HD ** (-0.5)
    head_id = ids_ref[0]
    shard_id = ids_ref[1]
    k = jnp.concatenate([kw_ref[...], kb_ref[...]], axis=0)
    v = jnp.concatenate([vw_ref[...], vb_ref[...]], axis=0)
    key_count = k.shape[0]
    row = lax.broadcasted_iota(jnp.int32, (rows, key_count), 0) + head_id * rows
    col = lax.broadcasted_iota(jnp.int32, (rows, key_count), 1)
    in_window = col < window
    visible = (in_window & (row >= col)) | (
        jnp.logical_not(in_window) & (col < window + shard_id * per_shard)
    )
    hidden = jnp.where(visible, 0.0, NEG_FILL).astype(jnp.float32)
    hidden = jnp.concatenate([hidden] * group_size, axis=0)
    nt = (((1,), (1,)), ((), ()))
    tn = (((0,), (0,)), ((), ()))
    q = jnp.concatenate([q_ref[:, g * HD:(g + 1) * HD] for g in range(group_size)], axis=0)
    do = jnp.concatenate([g_ref[:, g * HD:(g + 1) * HD] for g in range(group_size)], axis=0)
    scores = lax.dot_general(q, k, nt, preferred_element_type=jnp.float32) * scaling
    scores = scores + hidden
    row_max = jnp.max(scores, axis=1, keepdims=True)
    weights = jnp.exp(scores - row_max)
    probs = weights / jnp.sum(weights, axis=1, keepdims=True)
    probs_low = probs.astype(jnp.bfloat16)
    attended = jnp.dot(probs_low, v, preferred_element_type=jnp.float32).astype(jnp.bfloat16)
    row_dot = jnp.sum(do.astype(jnp.float32) * attended.astype(jnp.float32), axis=1, keepdims=True)
    dprob = lax.dot_general(do, v, nt, preferred_element_type=jnp.float32)
    grad_scores = (probs * (dprob - row_dot)).astype(jnp.bfloat16)
    query_grad = (
        jnp.dot(grad_scores, k, preferred_element_type=jnp.float32) * scaling
    ).astype(jnp.bfloat16)
    for g in range(group_size):
        att_ref[:, g * HD:(g + 1) * HD] = attended[g * rows:(g + 1) * rows]
        dq_ref[:, g * HD:(g + 1) * HD] = query_grad[g * rows:(g + 1) * rows]
    key_grad = (lax.dot_general(q, grad_scores, tn, preferred_element_type=jnp.float32) * scaling).T
    value_grad = lax.dot_general(do, probs_low, tn, preferred_element_type=jnp.float32).T
    wgrad_ref[:, :HD] = key_grad[:window]
    wgrad_ref[:, HD:] = value_grad[:window]
    bgrad_ref[:, :HD] = key_grad[window:].astype(jnp.bfloat16)
    bgrad_ref[:, HD:] = value_grad[window:].astype(jnp.bfloat16)


def attend_all(ids, queries, out_grad, kv_window, kv_beacons, per_shard, part, parts, earlier):
    rows, q_width = queries.shape
    q_width = q_width // parts
    window, kv_double = kv_window.shape
    beacon_total = kv_beacons.shape[0]
    kv_heads = kv_double // 2 // HD
    group_size = q_width // HD // kv_heads
    kernel = functools.partial(
        attention_kernel, rows=rows, window=window, per_shard=per_shard, group_size=group_size
    )
    qinblock = pl.BlockSpec((rows, group_size * HD), lambda h, ids: (0, h + part * kv_heads))
    qblock = pl.BlockSpec((rows, group_size * HD), lambda h, ids: (0, h + part * kv_heads))
    kwblock = pl.BlockSpec((window, HD), lambda h, ids: (0, h))
    vwblock = pl.BlockSpec((window, HD), lambda h, ids: (0, h + kv_heads))
    kbblock = pl.BlockSpec((beacon_total, HD), lambda h, ids: (0, h))
    vbblock = pl.BlockSpec((beacon_total, HD), lambda h, ids: (0, h + kv_heads))
    wgblock = pl.BlockSpec((window, 2 * HD), lambda h, ids: (0, h))
    bgblock = pl.BlockSpec((beacon_total, 2 * HD), lambda h, ids: (0, h))
    return pl.pallas_call(
        kernel,
        grid_spec=pltpu.PrefetchScalarGridSpec(
            num_scalar_prefetch=1,
            grid=(kv_heads,),
            in_specs=[qinblock, qinblock, kwblock, vwblock, kbblock, vbblock]
            + [pl.BlockSpec(memory_space=pl.ANY) for _ in earlier],
            out_specs=[wgblock, bgblock, qblock, qblock],
        ),
        out_shape=[
            jax.ShapeDtypeStruct((window, kv_double), jnp.float32),
            jax.ShapeDtypeStruct((beacon_total, kv_double), jnp.bfloat16),
            jax.ShapeDtypeStruct((rows, q_width * parts), jnp.bfloat16),
            jax.ShapeDtypeStruct((rows, q_width * parts), jnp.bfloat16),
        ],
        input_output_aliases={7 + i: 2 + i for i in range(len(earlier))},
    )(ids, queries, out_grad, kv_window, kv_window, kv_beacons, kv_beacons, *earlier)


def head_gather(block, axis, count):
    index = lax.axis_index(axis)
    from_left, from_right = [block], [block]
    for step in range(1, count):
        from_left.append(
            lax.ppermute(from_left[-1], axis, [(j, j + 1) for j in range(step - 1, count - 1)])
        )
        from_right.append(
            lax.ppermute(from_right[-1], axis, [(j + 1, j) for j in range(count - step)])
        )
    pieces = jnp.stack(from_left + from_right[1:])
    window = []
    for order in range(count):
        pick = jnp.where(order <= index, index - order, count - 1 + order - index)
        window.append(lax.dynamic_index_in_dim(pieces, pick, 0, keepdims=False))
    return jnp.concatenate(window, axis=0)


def head_reduce(partials, axis, count):
    index = lax.axis_index(axis)
    rows = partials.shape[0] // count

    def block_of(target):
        return lax.dynamic_slice_in_dim(partials, jnp.clip(target, 0, count - 1) * rows, rows, 0)

    left = jnp.zeros((rows, partials.shape[1]), jnp.bfloat16)
    right = jnp.zeros((rows, partials.shape[1]), jnp.bfloat16)
    for step in range(1, count):
        send_left = (block_of(index + step - count) + left.astype(jnp.float32)).astype(jnp.bfloat16)
        send_right = (block_of(index - step + count) + right.astype(jnp.float32)).astype(jnp.bfloat16)
        left = lax.ppermute(send_left, axis, [(j, j - 1) for j in range(max(1, count - step), count)])
        right = lax.ppermute(send_right, axis, [(j, j + 1) for j in range(0, min(step, count - 1))])
    return block_of(index) + left.astype(jnp.float32) + right.astype(jnp.float32)


def local_part(queries, keys, values, out_grad, positions, ids, heads_axis, ctx_axis, part, parts, earlier):
    kv_width = keys.shape[1]
    per_shard = positions.shape[0]
    kv_rows = jnp.concatenate([keys, values], axis=1)
    kv_window = head_gather(kv_rows, "head", heads_axis)
    window = kv_window.shape[0]
    own_beacon_rows = kv_window[jnp.tile(positions, ctx_axis)]
    kv_beacons = lax.all_to_all(
        own_beacon_rows.reshape(ctx_axis, per_shard, 2 * kv_width), "ctx", 0, 0, tiled=True,
    ).reshape(ctx_axis * per_shard, 2 * kv_width)
    window_grads, beacon_grads, attended_out, query_out = attend_all(
        ids, queries, out_grad, kv_window, kv_beacons, per_shard, part, parts, earlier
    )
    beacon_parts = lax.all_to_all(
        beacon_grads.reshape(ctx_axis, per_shard, 2 * kv_width), "ctx", 0, 0, tiled=True
    )
    own_beacons = jnp.sum(beacon_parts.astype(jnp.float32), axis=0)
    window_grads = window_grads.at[positions].add(own_beacons)
    own_grads = head_reduce(window_grads, "head", heads_axis).astype(jnp.bfloat16)
    own_grads = own_grads.reshape(own_grads.shape[0], kv_width // HD, 2, HD)
    rows = own_grads.shape[0]
    return (
        attended_out, query_out,
        own_grads[:, :, 0].reshape(rows, kv_width), own_grads[:, :, 1].reshape(rows, kv_width),
    )


def local(queries, keys, values, out_grad, beacon_pos, *, heads_axis, ctx_axis, parts):
    head_id = lax.axis_index("head")
    shard_id = lax.axis_index("ctx")
    ids = jnp.stack([head_id, shard_id]).astype(jnp.int32)
    positions = beacon_pos[0]
    q_cols = queries.shape[1] // parts
    kv_cols = keys.shape[1] // parts
    results = []
    for part in range(parts):
        qs = slice(part * q_cols, (part + 1) * q_cols)
        ks = slice(part * kv_cols, (part + 1) * kv_cols)
        results.append(
            local_part(
                queries, keys[:, ks], values[:, ks], out_grad,
                positions, ids, heads_axis, ctx_axis, part, parts,
                results[-1][:2] if results else (),
            )
        )
    key_grad, value_grad = (jnp.concatenate(outs, axis=1) for outs in list(zip(*results))[2:])
    return results[-1][0], results[-1][1], key_grad, value_grad


def solution(mesh):
    in_specs = (
        P(("ctx", "head"), None),
        P(("ctx", "head"), None),
        P(("ctx", "head"), None),
        P(("ctx", "head"), None),
        P("ctx", None),
    )
    out_specs = (
        P(("ctx", "head"), None),
        P(("ctx", "head"), None),
        P(("ctx", "head"), None),
        P(("ctx", "head"), None),
    )
    body = functools.partial(local, heads_axis=mesh.shape["head"], ctx_axis=mesh.shape["ctx"], parts=2)
    return jax.shard_map(body, mesh=mesh, in_specs=in_specs, out_specs=out_specs, check_vma=False)
```
